256 devices in a mesh: req: 32 (over y, x, core), tp: 8 (over z).
Axes of the slice: x: 4, y: 4, z: 8, core: 2. Of those that a mesh axis runs over, the one named last changes fastest.
Arguments:
- queries: bfloat16 [2048, 4096], P('req', 'tp'), may hold values from -8 to 8
- suffix_kv: bfloat16 [2048, 2, 1024], P('req', None, 'tp'), may hold values from -6 to 6
- prefix_cache: bfloat16 [32, 2048, 2, 1024], P('req', None, None, 'tp'), may hold values from -8 to 8
- prefix_owner: int32 [4], replicated, may hold values from 0 to 31, as said below
- request_prefix: int32 [64], P('req'), may hold values from 0 to 3
- suffix_len: int32 [64], P('req'), may hold values from 1 to 32, 1728 in all
- residual: bfloat16 [2048, 4096], P('req'), may hold values from -40 to 40
- norm_gain: float32 [4096], replicated, may hold values from 0.1 to 1.9
- router: float32 [4096, 8], replicated, may hold values from -0.09375 to 0.09375
- routes: int32 [2048, 2], P('req'), may hold values from 0 to 7, all different within a row; in each aligned block of 64 rows (0 to 63, 64 to 127, ...) at most 18 rows name the same one
- w_gate: bfloat16 [32, 4096, 2048], P('req', None, 'tp'), may hold values from -0.09375 to 0.09375
- w_up: bfloat16 [32, 4096, 2048], P('req', None, 'tp'), may hold values from -0.09375 to 0.09375
- w_down: bfloat16 [32, 2048, 4096], P('req', 'tp'), may hold values from -0.0625 to 0.0625
- w_out: bfloat16 [4096, 4096], P('tp'), may hold values from -1 to 1
Outputs:
- layer_out: bfloat16 [2048, 4096], P('req', 'tp')
The draws below stay inside these ranges and needn't reach their ends.
Inputs may be any that keep to these rules, and one draw needn't show every extreme that they name: `prefix_owner`: the 4 owners are distinct. Among the 64 token slots of one req index, no expert is named by more than 18 routes, and in some req indices one expert is named by exactly 18; the two experts of a token differ.
All inputs are finite; a program needn't handle non-finite values. No bound on the sum of `suffix_len` on one device may be relied on, other than what follows from the above.
Results may differ from the reference program's by a relative error of at most 0.017.
Values may be sent and summed in bfloat16 or wider, within the bound.
No kernel may reach another device: no remote copies, remote signals or barrier semaphores. Data moves between devices by JAX's collectives and lax.ppermute only.
A program may use at most 128 MiB of HBM per device.

```python
import math
import jax
import jax.numpy as jnp
import numpy as np
from jax import lax

D = 4096
HEADS = 32
KVH = 8
HD = 128
EXPERTS = 8
TOPK = 2
FF = 8192
RQ = 2
NPFX = 4
PLEN = 2048
SLOT = 32
NREQS = 64
TOKS = 2048
TOTAL_LEN = 1728
GROUPS = 4
FFQ = 2048
CAP = 18
N_REQ = 32
N_TP = 8


def draw_queries(key, part):
    noise_key = jax.random.fold_in(key, 1)
    values_field = jnp.clip(jax.random.normal(noise_key, (TOKS, HEADS * HD), jnp.float32), -6.0, 6.0)
    return values_field.astype(jnp.bfloat16)


def draw_prefix_cache(key, part):
    noise_key = jax.random.fold_in(key, 2)
    array_shape = (N_REQ, PLEN, 2, KVH * HD)
    values_field = jnp.clip(jax.random.normal(noise_key, array_shape, jnp.float32), -6.0, 6.0)
    return values_field.astype(jnp.bfloat16)


def draw_prefix_owner(key, part):
    others = jax.random.permutation(jax.random.fold_in(key, 3), N_REQ - 1)[:NPFX - 1].astype(jnp.int32)
    owners = jnp.concatenate([others, jnp.full((1,), N_REQ - 1, jnp.int32)])
    order = jax.random.permutation(jax.random.fold_in(key, 7), NPFX).astype(jnp.int32)
    return owners[order].astype(jnp.int32)


def draw_residual(key, part):
    base_key = jax.random.fold_in(key, 4)
    row_key = jax.random.fold_in(key, 5)
    rough_key = jax.random.fold_in(key, 6)
    columns = jnp.arange(D, dtype=jnp.float32) / (D - 1)
    base_field = jnp.clip(jax.random.normal(base_key, (TOKS, D), jnp.float32), -4.0, 4.0)
    row_scale = jnp.exp(jax.random.uniform(row_key, (TOKS,), jnp.float32, math.log(0.1), math.log(1.0)))
    column_scale = 3.0 ** columns
    roughness = jax.random.uniform(rough_key, (TOKS, D), jnp.float32, 0.5, 1.5)
    return (base_field * row_scale[:, None] * column_scale[None, :] * roughness).astype(jnp.bfloat16)


def with_ends(entries, stream_key, least, high):
    longest = entries.shape.index(max(entries.shape))
    spots = []
    for shift in (0, 1):
        where = [jax.random.randint(jax.random.fold_in(stream_key, axis), (), 0, length) for axis, length in enumerate(entries.shape)]
        where[longest] = (where[longest] + shift) % entries.shape[longest]
        spots.append(tuple(where))
    return entries.at[spots[0]].set(least).at[spots[1]].set(high)


def levels(own_key, dims, cuts, least, high):
    def one(dim, blocks):
        steps = jax.random.uniform(jax.random.fold_in(jax.random.fold_in(own_key, 6), dim), (blocks,), jnp.float32, least / len(cuts), high / len(cuts))
        return jnp.repeat(jnp.exp(steps), dims[dim] // blocks).reshape((-1,) + (1,) * (len(dims) - dim - 1))

    loudness = one(*cuts[0])
    for cut in cuts[1:]:
        loudness = loudness * one(*cut)
    return loudness


def cumulative_ranks(number_of, lean):
    portions = [(1 << 20) // math.isqrt(standing ** lean) + 1 for standing in range(1, number_of + 1)]
    scale = 1 + sum(portions) // (1 << 30)
    return np.cumsum(np.array([max(1, weight // scale) for weight in portions]))


def skewed_ids(own_key, dims, count, slope):
    grid = cumulative_ranks(count, slope)
    ticket = jax.random.randint(jax.random.fold_in(own_key, 1), dims, 0, int(grid[count - 1]))
    rank = jnp.searchsorted(jnp.asarray(grid, jnp.int32), ticket, side="right")
    return jax.random.permutation(jax.random.fold_in(own_key, 2), count)[rank].astype(jnp.int32)


def length_profile(amount, total, bound, lean):
    portions = [(1 << 20) // math.isqrt(standing ** lean) + 1 for standing in range(2, amount + 1)]
    rest, counts = total - bound - (amount - 1), [1] * (amount - 1)
    while rest > 0:
        free = [i for i in range(amount - 1) if counts[i] < bound]
        pool, budget = sum([portions[i] for i in free]), rest
        for i in free:
            extra = min(bound - counts[i], max(1, budget * portions[i] // pool), rest)
            counts[i] = counts[i] + extra
            rest = rest - extra
    return np.array([bound] + counts)


def uneven_parts(key, amount, total, reach, slope):
    if amount == 2:
        one = jax.random.randint(key, (), max(1, total - reach), min(reach, total - 1) + 1)
        return jnp.stack([one, total - one])
    lengths = jnp.asarray(length_profile(amount, total, reach, slope), jnp.int32)
    couples = (amount - 1) // 2
    donor, taker = lengths[1:1 + 2 * couples:2], lengths[2:2 + 2 * couples:2]
    margin = jnp.minimum(donor - 1, reach - taker)
    shifted = jax.random.randint(jax.random.fold_in(key, 1), (couples,), 0, 1 << 20) % (margin + 1)
    lengths = lengths.at[1:1 + 2 * couples:2].set(donor - shifted).at[2:2 + 2 * couples:2].set(taker + shifted)
    return lengths[jax.random.permutation(jax.random.fold_in(key, 2), amount)]


def assign_block(rng, own, number, rows, number_of, top, limit, lean):
    order = jax.random.permutation(rng, number_of)
    packed, usual = portions_of(number_of, rows * top, limit, lean, True), portions_of(number_of, rows * top, limit, lean, False)
    places = jnp.arange(number_of)

    def named(tallies, turn):
        used = int((tallies > 0).sum())
        fixed = max(1, used // 4)
        passed = fixed + (places - fixed + turn * (used - fixed)) % max(1, number_of - fixed)
        return jnp.zeros((number_of,), jnp.int32).at[order[jnp.where(places < fixed, places, passed)]].set(jnp.asarray(tallies, jnp.int32))

    tallies = jnp.where(number % 4 == 0, named(packed, number // 4), named(usual, number - number // 4 - 1))
    mixed = jax.random.permutation(jax.random.fold_in(own, 3), number_of)
    source_of, taker = mixed[0:number_of // 2 * 2:2], mixed[1:number_of // 2 * 2:2]
    room = jnp.minimum(tallies[source_of] - 1, limit - tallies[taker]) // 2
    room = jnp.where((source_of == order[0]) | (taker == order[0]) | (tallies[taker] == 0), 0, jnp.maximum(room, 0))
    passed = jax.random.randint(jax.random.fold_in(own, 4), (number_of // 2,), 0, 1 << 20) % (room + 1)
    tallies = tallies.at[source_of].add(-passed).at[taker].add(passed)
    labels = jnp.searchsorted(jnp.cumsum(tallies), jnp.arange(rows * top), side="right").astype(jnp.int32)
    grid = labels.reshape(top, rows).T
    grid = grid[jax.random.permutation(jax.random.fold_in(own, 1), rows)]
    turn = jax.random.randint(jax.random.fold_in(own, 2), (rows, 1), 0, top)
    return jnp.take_along_axis(grid, (jnp.arange(top)[None, :] + turn) % top, axis=1)


def portions_of(count, total, bound, lean, full):
    weights = [(1 << 20) // math.isqrt(rank ** lean) + 1 for rank in range(1, count + 1)]
    largest = bound if full else min(bound, max(-(-total // count), total * weights[0] // sum(weights)))
    least = 1 if total - largest >= count - 1 else 0
    counts, surplus = [largest] + [least] * (count - 1), total - largest - least * (count - 1)
    while surplus > 0:
        candidates = [i for i in range(1, count) if counts[i] < largest] or [i for i in range(1, count) if counts[i] < bound]
        mass, remaining = sum([weights[i] for i in candidates]), surplus
        for i in candidates:
            more = min(bound - counts[i], max(1, remaining * weights[i] // mass), surplus)
            counts[i] = counts[i] + more
            surplus = surplus - more
    return np.array(counts)


def centred(own_key, dims, width, most, shards=(), kind=jnp.bfloat16):
    level = levels(own_key, dims, shards, -0.22, 0.18) if shards else 1.0
    entries = jax.random.normal(own_key, dims, jnp.float32) * width * level
    return jnp.minimum(jnp.maximum(entries, -most), most).astype(kind)


def setup_inputs(seed: int = 0) -> dict:
    arg_keys = jax.random.split(jax.random.key(seed), 15)
    queries = draw_queries(jax.random.fold_in(arg_keys[14], 71), 0)
    suffix_kv = centred(arg_keys[1], (TOKS, 2, KVH * HD), 1.0, 6.0, ((0, 32), (2, 8)))
    prefix_cache = draw_prefix_cache(jax.random.fold_in(arg_keys[14], 71), 0)
    prefix_owner = draw_prefix_owner(jax.random.fold_in(arg_keys[14], 71), 0)
    request_prefix = with_ends(skewed_ids(arg_keys[4], (NREQS,), NPFX, 2), jax.random.fold_in(arg_keys[4], 3), 0, NPFX - 1).astype(jnp.int32)
    suffix_len = uneven_parts(arg_keys[5], NREQS, TOTAL_LEN, SLOT, 2).astype(jnp.int32)
    residual = draw_residual(jax.random.fold_in(arg_keys[14], 71), 0)
    norm_gain = jnp.clip(1.0 + 0.18 * jax.random.normal(arg_keys[7], (D,), jnp.float32), 0.1, 1.9)
    router = centred(arg_keys[8], (D, EXPERTS), D ** -0.5, 0.09375, (), jnp.float32)
    routes_keys = jax.random.split(jax.random.fold_in(arg_keys[9], 1), TOKS // (RQ * SLOT))
    routes_turns = jax.random.permutation(jax.random.fold_in(arg_keys[9], 3), TOKS // (RQ * SLOT))
    routes = jax.vmap(lambda own, number: assign_block(jax.random.fold_in(arg_keys[9], 2), own, number, RQ * SLOT, EXPERTS, TOPK, CAP, 2))(routes_keys, routes_turns).reshape((TOKS, TOPK))
    w_gate = centred(arg_keys[10], (N_REQ, D, FFQ), D ** -0.5, 0.09375, ((0, 32), (2, 8)))
    w_up = centred(arg_keys[11], (N_REQ, D, FFQ), D ** -0.5, 0.09375, ((0, 32), (2, 8)))
    w_down = centred(arg_keys[12], (N_REQ, FFQ, D), FF ** -0.5, 0.0625, ((0, 32), (1, 8)))
    w_out = centred(arg_keys[13], (HEADS * HD, D), HEADS ** -0.5, 1.0, ((0, 8),))
    return dict(queries=queries, suffix_kv=suffix_kv, prefix_cache=prefix_cache, prefix_owner=prefix_owner, request_prefix=request_prefix, suffix_len=suffix_len, residual=residual, norm_gain=norm_gain, router=router, routes=routes, w_gate=w_gate, w_up=w_up, w_down=w_down, w_out=w_out)


def rounded_f32(values):
    return lax.optimization_barrier(values.astype(jnp.bfloat16)).astype(jnp.float32)

def attend_block(query_block, suffix_block, cache_block, length):
    score_scale = 1.0 / math.sqrt(HD)
    prefix_score = jnp.einsum('ikgd,jkd->kgij', query_block, cache_block[:, 0]) * score_scale
    suffix_score = jnp.einsum('ikgd,jkd->kgij', query_block, suffix_block[:, 0]) * score_scale
    positions = jnp.arange(SLOT, dtype=jnp.int32)
    allowed = (positions[None, :] <= positions[:, None]) & (positions[None, :] < length)
    suffix_score = jnp.where(allowed, suffix_score, -1e+30)
    score_peak = jnp.maximum(prefix_score.max(-1), suffix_score.max(-1))[..., None]
    prefix_exp = jnp.exp(prefix_score - score_peak)
    suffix_exp = jnp.exp(suffix_score - score_peak)
    normaliser = prefix_exp.sum(-1, keepdims=True) + suffix_exp.sum(-1, keepdims=True)
    prefix_prob = rounded_f32(prefix_exp / normaliser)
    suffix_prob = rounded_f32(suffix_exp / normaliser)
    mixed_values = jnp.einsum('kgij,jkd->ikgd', prefix_prob, cache_block[:, 1])
    mixed_values = mixed_values + jnp.einsum('kgij,jkd->ikgd', suffix_prob, suffix_block[:, 1])
    return mixed_values

def reference(queries, suffix_kv, prefix_cache, prefix_owner, request_prefix, suffix_len, residual, norm_gain, router, routes, w_gate, w_up, w_down, w_out):
    group_size = HEADS // KVH
    cache_rows = prefix_owner[request_prefix].astype(jnp.int32)

    def one_request(request_index):
        row_start = (request_index * SLOT).astype(jnp.int32)
        query_block = lax.dynamic_slice_in_dim(queries, row_start, SLOT, 0).astype(jnp.float32).reshape(SLOT, KVH, group_size, HD)
        suffix_block = lax.dynamic_slice_in_dim(suffix_kv, row_start, SLOT, 0).astype(jnp.float32).reshape(SLOT, 2, KVH, HD)
        cache_block = prefix_cache[cache_rows[request_index]].astype(jnp.float32).reshape(PLEN, 2, KVH, HD)
        mixed_values = attend_block(query_block, suffix_block, cache_block, suffix_len[request_index])
        return mixed_values.reshape(SLOT, HEADS * HD).astype(jnp.bfloat16)
    attended = lax.map(one_request, jnp.arange(NREQS, dtype=jnp.int32)).reshape(TOKS, HEADS * HD)
    hidden_state = residual.astype(jnp.float32) + jnp.dot(attended, w_out, preferred_element_type=jnp.float32)
    inverse = lax.rsqrt(lax.optimization_barrier(jnp.mean(hidden_state * hidden_state, axis=1, keepdims=True)) + 1e-05)
    scaled = hidden_state * norm_gain.astype(jnp.float32) * inverse
    normed = scaled.astype(jnp.bfloat16)
    logits = jnp.dot(scaled, router, precision=lax.Precision.HIGHEST)
    picked_logit = jnp.take_along_axis(logits, routes, axis=1)
    first_weight = jax.nn.sigmoid(picked_logit[:, 0] - picked_logit[:, 1])
    route_weight = jnp.stack([first_weight, 1.0 - first_weight], axis=1)
    live_rows = jnp.arange(TOKS, dtype=jnp.int32) % SLOT < jnp.repeat(suffix_len, SLOT)
    pieces = GROUPS * N_TP
    piece_width = FF // pieces
    capacity_rows = N_REQ * CAP
    mixture = jnp.zeros((TOKS, D), jnp.float32)
    for expert in range(EXPERTS):
        picked = (routes == expert) & live_rows[:, None]
        flagged = jnp.any(picked, axis=1)
        weight_sum = lax.optimization_barrier(jnp.sum(jnp.where(picked, route_weight, 0.0), axis=1))
        ordering = jnp.argsort(jnp.where(flagged, 0, 1).astype(jnp.int32), stable=True)[:capacity_rows].astype(jnp.int32)
        picked_rows = normed[ordering]
        gate_matrix = jnp.transpose(w_gate[expert::EXPERTS], (1, 0, 2)).reshape(D, FF)
        up_matrix = jnp.transpose(w_up[expert::EXPERTS], (1, 0, 2)).reshape(D, FF)
        down_blocks = w_down[expert::EXPERTS].reshape(pieces, piece_width, D)
        gate_value = jnp.dot(picked_rows, gate_matrix, preferred_element_type=jnp.float32)
        up_value = jnp.dot(picked_rows, up_matrix, preferred_element_type=jnp.float32)
        hidden_units = (jax.nn.silu(gate_value) * up_value).astype(jnp.bfloat16)
        hidden_blocks = jnp.transpose(hidden_units.reshape(capacity_rows, pieces, piece_width), (1, 0, 2))

        def add_block(running, pair_item):
            hidden_block, down_block = pair_item
            piece_out = jnp.dot(hidden_block, down_block, preferred_element_type=jnp.float32)
            return (running + rounded_f32(piece_out), None)
        expert_out, _ = lax.scan(add_block, jnp.zeros((capacity_rows, D), jnp.float32), (hidden_blocks, down_blocks))
        factor = jnp.where(flagged[ordering], weight_sum[ordering], 0.0)
        mixture = mixture.at[ordering].add(factor[:, None] * expert_out)
    layer_out = jnp.where(live_rows[:, None], hidden_state + mixture, 0.0)
    return layer_out.astype(jnp.bfloat16)
```

```python
import math

import jax
import jax.numpy as jnp
from jax import lax
from jax.sharding import PartitionSpec as P

HEADS = 32
KVH = 8
HD = 128
EXPERTS = 8
NPFX = 4
CAP = 18


def broadcast(x, axis, root):
    mine = lax.axis_index(axis) == root
    return lax.psum(jnp.where(mine, x, jnp.zeros_like(x)), axis)


def fetch_prefixes(prefix_cache, prefix_owner, request_prefix, req_count):
    plen = prefix_cache.shape[1]
    width = prefix_cache.shape[3]
    piece = plen // req_count
    requests = request_prefix.shape[0]
    pieces = prefix_cache.reshape(req_count, piece, 2, width)
    scattered = lax.all_to_all(pieces, "req", 0, 0, tiled=True)
    owner_pieces = jnp.take(scattered, prefix_owner, axis=0)
    wanted = lax.all_to_all(
        jnp.broadcast_to(request_prefix[None], (req_count, requests)), "req", 0, 0, tiled=True
    )
    outgoing = jnp.take(owner_pieces, wanted.reshape(-1), axis=0).reshape(
        req_count, requests, piece, 2, width
    )
    arrived = lax.all_to_all(outgoing, "req", 0, 0, tiled=True)
    return jnp.transpose(arrived, (1, 0, 2, 3, 4)).reshape(requests, plen, 2, width)


def tp_reduce_scatter(values, tp_count):
    rows, width = values.shape
    share = width // tp_count
    chunks = jnp.transpose(
        values.astype(jnp.bfloat16).reshape(rows, tp_count, share), (1, 0, 2)
    )
    arrived = lax.all_to_all(chunks, "tp", 0, 0, tiled=True)
    return arrived.astype(jnp.float32).sum(axis=0)


def tp_all_gather(share_values, tp_count):
    rows, share = share_values.shape
    copies = jnp.broadcast_to(share_values[None], (tp_count, rows, share))
    arrived = lax.all_to_all(copies, "tp", 0, 0, tiled=True)
    return jnp.transpose(arrived, (1, 0, 2)).reshape(rows, tp_count * share)


def attend_local(queries, suffix_kv, chosen, suffix_len, requests, slot_len):
    kv_local = suffix_kv.shape[2] // HD
    group_size = HEADS // KVH
    plen_local = chosen.shape[1]
    query_block = queries.reshape(requests, slot_len, kv_local, group_size, HD)
    cache_block = chosen.reshape(requests, plen_local, 2, kv_local, HD)
    suffix_block = suffix_kv.reshape(requests, slot_len, 2, kv_local, HD)
    score_scale = 1.0 / math.sqrt(HD)
    prefix_score = (
        jnp.einsum(
            "rikgd,rjkd->rkgij",
            query_block,
            cache_block[:, :, 0],
            preferred_element_type=jnp.float32,
        )
        * score_scale
    )
    suffix_score = (
        jnp.einsum(
            "rikgd,rjkd->rkgij",
            query_block,
            suffix_block[:, :, 0],
            preferred_element_type=jnp.float32,
        )
        * score_scale
    )
    positions = jnp.arange(slot_len, dtype=jnp.int32)
    allowed = (positions[None, None, :] <= positions[None, :, None]) & (
        positions[None, None, :] < suffix_len[:, None, None]
    )
    suffix_score = jnp.where(allowed[:, None, None], suffix_score, -1e30)
    score_peak = jnp.maximum(prefix_score.max(-1), suffix_score.max(-1))[..., None]
    prefix_exp = jnp.exp(prefix_score - score_peak)
    suffix_exp = jnp.exp(suffix_score - score_peak)
    normaliser = prefix_exp.sum(-1, keepdims=True) + suffix_exp.sum(-1, keepdims=True)
    prefix_prob = (prefix_exp / normaliser).astype(jnp.bfloat16)
    suffix_prob = (suffix_exp / normaliser).astype(jnp.bfloat16)
    mixed_values = jnp.einsum(
        "rkgij,rjkd->rikgd", prefix_prob, cache_block[:, :, 1], preferred_element_type=jnp.float32
    )
    mixed_values = mixed_values + jnp.einsum(
        "rkgij,rjkd->rikgd", suffix_prob, suffix_block[:, :, 1], preferred_element_type=jnp.float32
    )
    return mixed_values.reshape(requests * slot_len, kv_local * group_size * HD).astype(
        jnp.bfloat16
    )


def routing_tables(routes, live_rows, route_weight):
    expert_ids = jnp.arange(EXPERTS, dtype=jnp.int32)
    member = (routes[:, :, None] == expert_ids) & live_rows[:, None, None]
    member_int = member.astype(jnp.int32)
    flat_member = member_int.reshape(-1, EXPERTS)
    earlier = jnp.cumsum(flat_member, axis=0) - flat_member
    slot_index = jnp.sum(earlier * flat_member, axis=1).reshape(routes.shape)
    slot_hit = (slot_index[:, :, None] == jnp.arange(CAP, dtype=jnp.int32)).astype(jnp.float32)
    member_float = member.astype(jnp.float32)
    placing = (
        jnp.einsum("tke,tkc->ect", member_float, slot_hit)
        .reshape(EXPERTS * CAP, routes.shape[0])
        .astype(jnp.bfloat16)
    )
    combining = jnp.einsum(
        "tke,tkc,tk->tec", member_float, slot_hit, route_weight, precision=lax.Precision.HIGHEST
    )
    return (placing, combining.reshape(routes.shape[0], EXPERTS * CAP))


def expert_apply(arrived, w_gate, w_up, w_down):
    flat_rows = arrived.reshape(-1, arrived.shape[2])
    gate_value = jnp.dot(flat_rows, w_gate[0], preferred_element_type=jnp.float32)
    up_value = jnp.dot(flat_rows, w_up[0], preferred_element_type=jnp.float32)
    hidden_units = (jax.nn.silu(gate_value) * up_value).astype(jnp.bfloat16)
    piece_out = jnp.dot(hidden_units, w_down[0], preferred_element_type=jnp.float32).astype(
        jnp.bfloat16
    )
    return piece_out.reshape(arrived.shape[0], arrived.shape[1], piece_out.shape[1])


def send_back(parts):
    return lax.all_to_all(parts, "req", split_axis=0, concat_axis=0, tiled=True)


def per_device(
    queries,
    suffix_kv,
    prefix_cache,
    prefix_owner,
    request_prefix,
    suffix_len,
    residual,
    norm_gain,
    router,
    routes,
    w_gate,
    w_up,
    w_down,
    w_out,
):
    tp_count = lax.axis_size("tp")
    tp_index = lax.axis_index("tp")
    req_count = lax.axis_size("req")
    model_width = residual.shape[1]
    share_width = model_width // tp_count
    share_start = tp_index * share_width
    requests = request_prefix.shape[0]
    slot_len = queries.shape[0] // requests
    chosen = fetch_prefixes(prefix_cache, prefix_owner, request_prefix, req_count)
    attended = attend_local(queries, suffix_kv, chosen, suffix_len, requests, slot_len)
    partial_value = jnp.dot(attended, w_out, preferred_element_type=jnp.float32)
    attn_share = tp_reduce_scatter(partial_value, tp_count)
    attn_full = tp_all_gather(attn_share.astype(jnp.bfloat16), tp_count)
    hidden_state = residual.astype(jnp.float32) + attn_full.astype(jnp.float32)
    residual_share = lax.dynamic_slice_in_dim(residual, share_start, share_width, 1)
    hidden_share = residual_share.astype(jnp.float32) + attn_share
    inverse = lax.rsqrt(jnp.mean(hidden_state * hidden_state, axis=1, keepdims=True) + 1e-05)
    scaled = hidden_state * norm_gain * inverse
    logits = jnp.dot(scaled, router, precision=lax.Precision.HIGHEST)
    normed_full = scaled.astype(jnp.bfloat16)
    route_hit = (routes[:, :, None] == jnp.arange(EXPERTS, dtype=jnp.int32)).astype(jnp.float32)
    picked_logit = jnp.sum(route_hit * logits[:, None, :], axis=2)
    first_weight = jax.nn.sigmoid(picked_logit[:, 0] - picked_logit[:, 1])
    route_weight = jnp.stack([first_weight, 1.0 - first_weight], axis=1)
    live_rows = jnp.arange(routes.shape[0], dtype=jnp.int32) % slot_len < jnp.repeat(
        suffix_len, slot_len
    )
    placing, combining = routing_tables(routes, live_rows, route_weight)
    repeats = req_count // EXPERTS
    send_rows = jnp.dot(placing, normed_full, preferred_element_type=jnp.float32).astype(
        jnp.bfloat16
    )
    outgoing = jnp.tile(send_rows.reshape(EXPERTS, CAP, model_width), (repeats, 1, 1))
    returned = send_back(
        expert_apply(
            lax.all_to_all(outgoing, "req", split_axis=0, concat_axis=0, tiled=True),
            w_gate,
            w_up,
            w_down,
        )
    )
    summed = returned.astype(jnp.float32).reshape(repeats, EXPERTS, CAP, model_width).sum(axis=0)
    mixture_full = jnp.dot(
        combining, summed.reshape(EXPERTS * CAP, model_width), precision=lax.Precision.HIGHEST
    )
    mixture_share = tp_reduce_scatter(mixture_full, tp_count)
    layer_out = jnp.where(live_rows[:, None], hidden_share + mixture_share, 0.0)
    return layer_out.astype(jnp.bfloat16)


def solution(mesh):
    return jax.shard_map(
        per_device,
        mesh=mesh,
        in_specs=(
            P("req", "tp"),
            P("req", None, "tp"),
            P("req", None, None, "tp"),
            P(),
            P("req"),
            P("req"),
            P("req", None),
            P(),
            P(),
            P("req", None),
            P("req", None, "tp"),
            P("req", None, "tp"),
            P("req", "tp", None),
            P("tp", None),
        ),
        out_specs=P("req", "tp"),
        check_vma=False,
    )
```

```python
import math

import jax
import jax.numpy as jnp
from jax import lax
from jax.sharding import PartitionSpec as P

HEADS = 32
KVH = 8
HD = 128
EXPERTS = 8
NPFX = 4
CAP = 18
LANES = 128


def broadcast(x, axis, root):
    mine = lax.axis_index(axis) == root
    return lax.psum(jnp.where(mine, x, jnp.zeros_like(x)), axis)


def fetch_prefixes(prefix_cache, prefix_owner, request_prefix, req_count):
    plen = prefix_cache.shape[1]
    width = prefix_cache.shape[3]
    piece = plen // req_count
    requests = request_prefix.shape[0]
    pieces = prefix_cache.reshape(req_count, piece, 2, width)
    scattered = lax.all_to_all(pieces, "req", 0, 0, tiled=True)
    owner_pieces = jnp.take(scattered, prefix_owner, axis=0)
    wanted = lax.all_to_all(
        jnp.broadcast_to(request_prefix[None], (req_count, requests)), "req", 0, 0, tiled=True
    )
    outgoing = jnp.take(owner_pieces, wanted.reshape(-1), axis=0).reshape(
        req_count, requests, piece, 2, width
    )
    arrived = lax.all_to_all(outgoing, "req", 0, 0, tiled=True)
    return jnp.transpose(arrived, (1, 0, 2, 3, 4)).reshape(requests, plen, 2, width)


def tp_reduce_scatter(values, tp_count):
    rows, width = values.shape
    share = width // tp_count
    chunks = jnp.transpose(
        values.astype(jnp.bfloat16).reshape(rows, tp_count, share), (1, 0, 2)
    )
    arrived = lax.all_to_all(chunks, "tp", 0, 0, tiled=True)
    return arrived.astype(jnp.float32).sum(axis=0)


def tp_all_gather(share_values, tp_count):
    rows, share = share_values.shape
    copies = jnp.broadcast_to(share_values[None], (tp_count, rows, share))
    arrived = lax.all_to_all(copies, "tp", 0, 0, tiled=True)
    return jnp.transpose(arrived, (1, 0, 2)).reshape(rows, tp_count * share)


def attend_local(queries, suffix_kv, chosen, suffix_len, requests, slot_len):
    kv_local = suffix_kv.shape[2] // HD
    group_size = HEADS // KVH
    plen_local = chosen.shape[1]
    query_block = queries.reshape(requests, slot_len, kv_local, group_size, HD)
    cache_block = chosen.reshape(requests, plen_local, 2, kv_local, HD)
    suffix_block = suffix_kv.reshape(requests, slot_len, 2, kv_local, HD)
    score_scale = 1.0 / math.sqrt(HD)
    prefix_score = (
        jnp.einsum(
            "rikgd,rjkd->rkgij",
            query_block,
            cache_block[:, :, 0],
            preferred_element_type=jnp.float32,
        )
        * score_scale
    )
    suffix_score = (
        jnp.einsum(
            "rikgd,rjkd->rkgij",
            query_block,
            suffix_block[:, :, 0],
            preferred_element_type=jnp.float32,
        )
        * score_scale
    )
    positions = jnp.arange(slot_len, dtype=jnp.int32)
    allowed = (positions[None, None, :] <= positions[None, :, None]) & (
        positions[None, None, :] < suffix_len[:, None, None]
    )
    suffix_score = jnp.where(allowed[:, None, None], suffix_score, -1e30)
    score_peak = jnp.maximum(prefix_score.max(-1), suffix_score.max(-1))[..., None]
    prefix_exp = jnp.exp(prefix_score - score_peak)
    suffix_exp = jnp.exp(suffix_score - score_peak)
    normaliser = prefix_exp.sum(-1, keepdims=True) + suffix_exp.sum(-1, keepdims=True)
    prefix_prob = (prefix_exp / normaliser).astype(jnp.bfloat16)
    suffix_prob = (suffix_exp / normaliser).astype(jnp.bfloat16)
    mixed_values = jnp.einsum(
        "rkgij,rjkd->rikgd", prefix_prob, cache_block[:, :, 1], preferred_element_type=jnp.float32
    )
    mixed_values = mixed_values + jnp.einsum(
        "rkgij,rjkd->rikgd", suffix_prob, suffix_block[:, :, 1], preferred_element_type=jnp.float32
    )
    return mixed_values.reshape(requests * slot_len, kv_local * group_size * HD).astype(
        jnp.bfloat16
    )


def routing_tables(routes, live_rows, route_weight):
    expert_ids = jnp.arange(EXPERTS, dtype=jnp.int32)
    member = (routes[:, :, None] == expert_ids) & live_rows[:, None, None]
    member_int = member.astype(jnp.int32)
    flat_member = member_int.reshape(-1, EXPERTS)
    earlier = jnp.cumsum(flat_member, axis=0) - flat_member
    slot_index = jnp.sum(earlier * flat_member, axis=1).reshape(routes.shape)
    slot_hit = (slot_index[:, :, None] == jnp.arange(CAP, dtype=jnp.int32)).astype(jnp.float32)
    member_float = member.astype(jnp.float32)
    placing = (
        jnp.einsum("tke,tkc->ect", member_float, slot_hit)
        .reshape(EXPERTS * CAP, routes.shape[0])
        .astype(jnp.bfloat16)
    )
    combining = jnp.einsum(
        "tke,tkc,tk->tec", member_float, slot_hit, route_weight, precision=lax.Precision.HIGHEST
    )
    return (placing, combining.reshape(routes.shape[0], EXPERTS * CAP))


def expert_apply(arrived, w_gate, w_up, w_down):
    flat_rows = arrived.reshape(-1, w_gate.shape[1])
    gate_value = jnp.dot(flat_rows, w_gate[0], preferred_element_type=jnp.float32)
    up_value = jnp.dot(flat_rows, w_up[0], preferred_element_type=jnp.float32)
    hidden_units = (jax.nn.silu(gate_value) * up_value).astype(jnp.bfloat16)
    piece_out = jnp.dot(hidden_units, w_down[0], preferred_element_type=jnp.float32).astype(
        jnp.bfloat16
    )
    return piece_out.reshape(arrived.shape)


def send_back(parts):
    return lax.all_to_all(parts, "req", split_axis=0, concat_axis=0, tiled=True)


def per_device(
    queries,
    suffix_kv,
    prefix_cache,
    prefix_owner,
    request_prefix,
    suffix_len,
    residual,
    norm_gain,
    router,
    routes,
    w_gate,
    w_up,
    w_down,
    w_out,
):
    tp_count = lax.axis_size("tp")
    tp_index = lax.axis_index("tp")
    req_count = lax.axis_size("req")
    model_width = residual.shape[1]
    share_width = model_width // tp_count
    share_start = tp_index * share_width
    requests = request_prefix.shape[0]
    slot_len = queries.shape[0] // requests
    chosen = fetch_prefixes(prefix_cache, prefix_owner, request_prefix, req_count)
    attended = attend_local(queries, suffix_kv, chosen, suffix_len, requests, slot_len)
    partial_value = jnp.dot(attended, w_out, preferred_element_type=jnp.float32)
    attn_share = tp_reduce_scatter(partial_value, tp_count)
    attn_full = tp_all_gather(attn_share.astype(jnp.bfloat16), tp_count)
    hidden_state = residual.astype(jnp.float32) + attn_full.astype(jnp.float32)
    residual_share = lax.dynamic_slice_in_dim(residual, share_start, share_width, 1)
    hidden_share = residual_share.astype(jnp.float32) + attn_share
    inverse = lax.rsqrt(jnp.mean(hidden_state * hidden_state, axis=1, keepdims=True) + 1e-05)
    scaled = hidden_state * norm_gain * inverse
    logits = jnp.dot(scaled, router, precision=lax.Precision.HIGHEST)
    normed_full = scaled.astype(jnp.bfloat16)
    route_hit = (routes[:, :, None] == jnp.arange(EXPERTS, dtype=jnp.int32)).astype(jnp.float32)
    picked_logit = jnp.sum(route_hit * logits[:, None, :], axis=2)
    first_weight = jax.nn.sigmoid(picked_logit[:, 0] - picked_logit[:, 1])
    route_weight = jnp.stack([first_weight, 1.0 - first_weight], axis=1)
    live_rows = jnp.arange(routes.shape[0], dtype=jnp.int32) % slot_len < jnp.repeat(
        suffix_len, slot_len
    )
    placing, combining = routing_tables(routes, live_rows, route_weight)
    repeats = req_count // EXPERTS
    send_rows = jnp.dot(placing, normed_full, preferred_element_type=jnp.float32).astype(
        jnp.bfloat16
    )
    packed_rows = CAP * model_width // LANES
    outgoing = jnp.tile(send_rows.reshape(EXPERTS, packed_rows, LANES), (repeats, 1, 1))
    returned = send_back(
        expert_apply(
            lax.all_to_all(outgoing, "req", split_axis=0, concat_axis=0, tiled=True),
            w_gate,
            w_up,
            w_down,
        )
    )
    summed = returned.astype(jnp.float32).reshape(repeats, EXPERTS, packed_rows, LANES).sum(axis=0)
    mixture_full = jnp.dot(
        combining, summed.reshape(EXPERTS * CAP, model_width), precision=lax.Precision.HIGHEST
    )
    mixture_share = tp_reduce_scatter(mixture_full, tp_count)
    layer_out = jnp.where(live_rows[:, None], hidden_share + mixture_share, 0.0)
    return layer_out.astype(jnp.bfloat16)


def solution(mesh):
    return jax.shard_map(
        per_device,
        mesh=mesh,
        in_specs=(
            P("req", "tp"),
            P("req", None, "tp"),
            P("req", None, None, "tp"),
            P(),
            P("req"),
            P("req"),
            P("req", None),
            P(),
            P(),
            P("req", None),
            P("req", None, "tp"),
            P("req", None, "tp"),
            P("req", "tp", None),
            P("tp", None),
        ),
        out_specs=P("req", "tp"),
        check_vma=False,
    )
```

```python
import math

import jax
import jax.numpy as jnp
from jax import lax
from jax.sharding import PartitionSpec as P

HEADS = 32
KVH = 8
HD = 128
EXPERTS = 8
NPFX = 4
CAP = 18
LANES = 128
CHUNKS = 2


def broadcast(x, axis, root):
    mine = lax.axis_index(axis) == root
    return lax.psum(jnp.where(mine, x, jnp.zeros_like(x)), axis)


def fetch_prefixes(prefix_cache, prefix_owner, request_prefix, req_count):
    plen = prefix_cache.shape[1]
    width = prefix_cache.shape[3]
    piece = plen // req_count
    requests = request_prefix.shape[0]
    pieces = prefix_cache.reshape(req_count, piece, 2, width)
    scattered = lax.all_to_all(pieces, "req", 0, 0, tiled=True)
    owner_pieces = jnp.take(scattered, prefix_owner, axis=0)
    wanted = lax.all_to_all(
        jnp.broadcast_to(request_prefix[None], (req_count, requests)), "req", 0, 0, tiled=True
    )
    outgoing = jnp.take(owner_pieces, wanted.reshape(-1), axis=0).reshape(
        req_count, requests, piece, 2, width
    )
    arrived = lax.all_to_all(outgoing, "req", 0, 0, tiled=True)
    return jnp.transpose(arrived, (1, 0, 2, 3, 4)).reshape(requests, plen, 2, width)


def tp_reduce_scatter(values, tp_count):
    rows, width = values.shape
    share = width // tp_count
    chunks = jnp.transpose(
        values.astype(jnp.bfloat16).reshape(rows, tp_count, share), (1, 0, 2)
    )
    arrived = lax.all_to_all(chunks, "tp", 0, 0, tiled=True)
    return arrived.astype(jnp.float32).sum(axis=0)


def tp_all_gather(share_values, tp_count):
    rows, share = share_values.shape
    copies = jnp.broadcast_to(share_values[None], (tp_count, rows, share))
    arrived = lax.all_to_all(copies, "tp", 0, 0, tiled=True)
    return jnp.transpose(arrived, (1, 0, 2)).reshape(rows, tp_count * share)


def attend_local(queries, suffix_kv, chosen, suffix_len, requests, slot_len):
    kv_local = suffix_kv.shape[2] // HD
    group_size = HEADS // KVH
    plen_local = chosen.shape[1]
    query_block = queries.reshape(requests, slot_len, kv_local, group_size, HD)
    cache_block = chosen.reshape(requests, plen_local, 2, kv_local, HD)
    suffix_block = suffix_kv.reshape(requests, slot_len, 2, kv_local, HD)
    score_scale = 1.0 / math.sqrt(HD)
    prefix_score = (
        jnp.einsum(
            "rikgd,rjkd->rkgij",
            query_block,
            cache_block[:, :, 0],
            preferred_element_type=jnp.float32,
        )
        * score_scale
    )
    suffix_score = (
        jnp.einsum(
            "rikgd,rjkd->rkgij",
            query_block,
            suffix_block[:, :, 0],
            preferred_element_type=jnp.float32,
        )
        * score_scale
    )
    positions = jnp.arange(slot_len, dtype=jnp.int32)
    allowed = (positions[None, None, :] <= positions[None, :, None]) & (
        positions[None, None, :] < suffix_len[:, None, None]
    )
    suffix_score = jnp.where(allowed[:, None, None], suffix_score, -1e30)
    score_peak = jnp.maximum(prefix_score.max(-1), suffix_score.max(-1))[..., None]
    prefix_exp = jnp.exp(prefix_score - score_peak)
    suffix_exp = jnp.exp(suffix_score - score_peak)
    normaliser = prefix_exp.sum(-1, keepdims=True) + suffix_exp.sum(-1, keepdims=True)
    prefix_prob = (prefix_exp / normaliser).astype(jnp.bfloat16)
    suffix_prob = (suffix_exp / normaliser).astype(jnp.bfloat16)
    mixed_values = jnp.einsum(
        "rkgij,rjkd->rikgd", prefix_prob, cache_block[:, :, 1], preferred_element_type=jnp.float32
    )
    mixed_values = mixed_values + jnp.einsum(
        "rkgij,rjkd->rikgd", suffix_prob, suffix_block[:, :, 1], preferred_element_type=jnp.float32
    )
    return mixed_values.reshape(requests * slot_len, kv_local * group_size * HD).astype(
        jnp.bfloat16
    )


def routing_tables(routes, live_rows, route_weight):
    expert_ids = jnp.arange(EXPERTS, dtype=jnp.int32)
    member = (routes[:, :, None] == expert_ids) & live_rows[:, None, None]
    member_int = member.astype(jnp.int32)
    flat_member = member_int.reshape(-1, EXPERTS)
    earlier = jnp.cumsum(flat_member, axis=0) - flat_member
    slot_index = jnp.sum(earlier * flat_member, axis=1).reshape(routes.shape)
    slot_hit = (slot_index[:, :, None] == jnp.arange(CAP, dtype=jnp.int32)).astype(jnp.float32)
    member_float = member.astype(jnp.float32)
    placing = (
        jnp.einsum("tke,tkc->ect", member_float, slot_hit)
        .reshape(EXPERTS * CAP, routes.shape[0])
        .astype(jnp.bfloat16)
    )
    combining = jnp.einsum(
        "tke,tkc,tk->tec", member_float, slot_hit, route_weight, precision=lax.Precision.HIGHEST
    )
    return (placing, combining.reshape(routes.shape[0], EXPERTS * CAP))


def expert_apply(arrived, w_gate, w_up, w_down):
    flat_rows = arrived.reshape(-1, w_gate.shape[1])
    gate_value = jnp.dot(flat_rows, w_gate[0], preferred_element_type=jnp.float32)
    up_value = jnp.dot(flat_rows, w_up[0], preferred_element_type=jnp.float32)
    hidden_units = (jax.nn.silu(gate_value) * up_value).astype(jnp.bfloat16)
    piece_out = jnp.dot(hidden_units, w_down[0], preferred_element_type=jnp.float32).astype(
        jnp.bfloat16
    )
    return piece_out.reshape(arrived.shape)


def send_back(parts):
    return lax.all_to_all(parts, "req", split_axis=0, concat_axis=0, tiled=True)


def per_device(
    queries,
    suffix_kv,
    prefix_cache,
    prefix_owner,
    request_prefix,
    suffix_len,
    residual,
    norm_gain,
    router,
    routes,
    w_gate,
    w_up,
    w_down,
    w_out,
):
    tp_count = lax.axis_size("tp")
    tp_index = lax.axis_index("tp")
    req_count = lax.axis_size("req")
    model_width = residual.shape[1]
    share_width = model_width // tp_count
    share_start = tp_index * share_width
    requests = request_prefix.shape[0]
    slot_len = queries.shape[0] // requests
    chosen = fetch_prefixes(prefix_cache, prefix_owner, request_prefix, req_count)
    attended = attend_local(queries, suffix_kv, chosen, suffix_len, requests, slot_len)
    partial_value = jnp.dot(attended, w_out, preferred_element_type=jnp.float32)
    attn_share = tp_reduce_scatter(partial_value, tp_count)
    attn_full = tp_all_gather(attn_share.astype(jnp.bfloat16), tp_count)
    hidden_state = residual.astype(jnp.float32) + attn_full.astype(jnp.float32)
    residual_share = lax.dynamic_slice_in_dim(residual, share_start, share_width, 1)
    hidden_share = residual_share.astype(jnp.float32) + attn_share
    inverse = lax.rsqrt(jnp.mean(hidden_state * hidden_state, axis=1, keepdims=True) + 1e-05)
    scaled = hidden_state * norm_gain * inverse
    logits = jnp.dot(scaled, router, precision=lax.Precision.HIGHEST)
    normed_full = scaled.astype(jnp.bfloat16)
    route_hit = (routes[:, :, None] == jnp.arange(EXPERTS, dtype=jnp.int32)).astype(jnp.float32)
    picked_logit = jnp.sum(route_hit * logits[:, None, :], axis=2)
    first_weight = jax.nn.sigmoid(picked_logit[:, 0] - picked_logit[:, 1])
    route_weight = jnp.stack([first_weight, 1.0 - first_weight], axis=1)
    live_rows = jnp.arange(routes.shape[0], dtype=jnp.int32) % slot_len < jnp.repeat(
        suffix_len, slot_len
    )
    placing, combining = routing_tables(routes, live_rows, route_weight)
    repeats = req_count // EXPERTS
    tokens = routes.shape[0]
    chunk_slots = CAP // CHUNKS
    packed_rows = chunk_slots * model_width // LANES
    placing_blocks = placing.reshape(EXPERTS, CAP, tokens)
    combining_blocks = combining.reshape(tokens, EXPERTS, CAP)
    mixture_full = jnp.zeros((tokens, model_width), jnp.float32)
    for chunk in range(CHUNKS):
        slots = slice(chunk * chunk_slots, (chunk + 1) * chunk_slots)
        chunk_placing = placing_blocks[:, slots].reshape(EXPERTS * chunk_slots, tokens)
        send_rows = jnp.dot(chunk_placing, normed_full, preferred_element_type=jnp.float32).astype(
            jnp.bfloat16
        )
        outgoing = jnp.tile(send_rows.reshape(EXPERTS, packed_rows, LANES), (repeats, 1, 1))
        returned = send_back(
            expert_apply(
                lax.all_to_all(outgoing, "req", split_axis=0, concat_axis=0, tiled=True),
                w_gate,
                w_up,
                w_down,
            )
        )
        summed = returned.astype(jnp.float32).reshape(repeats, EXPERTS, packed_rows, LANES).sum(
            axis=0
        )
        mixture_full = mixture_full + jnp.dot(
            combining_blocks[:, :, slots].reshape(tokens, EXPERTS * chunk_slots),
            summed.reshape(EXPERTS * chunk_slots, model_width),
            precision=lax.Precision.HIGHEST,
        )
    mixture_share = tp_reduce_scatter(mixture_full, tp_count)
    layer_out = jnp.where(live_rows[:, None], hidden_share + mixture_share, 0.0)
    return layer_out.astype(jnp.bfloat16)


def solution(mesh):
    return jax.shard_map(
        per_device,
        mesh=mesh,
        in_specs=(
            P("req", "tp"),
            P("req", None, "tp"),
            P("req", None, None, "tp"),
            P(),
            P("req"),
            P("req"),
            P("req", None),
            P(),
            P(),
            P("req", None),
            P("req", None, "tp"),
            P("req", None, "tp"),
            P("req", "tp", None),
            P("tp", None),
        ),
        out_specs=P("req", "tp"),
        check_vma=False,
    )
```

```python
import math

import jax
import jax.numpy as jnp
from jax import lax
from jax.sharding import PartitionSpec as P

HEADS = 32
KVH = 8
HD = 128
EXPERTS = 8
NPFX = 4
CAP = 18
LANES = 128
CHUNKS = 2


def broadcast(x, axis, root):
    mine = lax.axis_index(axis) == root
    return lax.psum(jnp.where(mine, x, jnp.zeros_like(x)), axis)


def fetch_prefixes(prefix_cache, prefix_owner, request_prefix, req_count):
    plen = prefix_cache.shape[1]
    width = prefix_cache.shape[3]
    piece = plen // req_count
    requests = request_prefix.shape[0]
    pieces = prefix_cache.reshape(req_count, piece, 2, width)
    scattered = lax.all_to_all(pieces, "req", 0, 0, tiled=True)
    owner_pieces = jnp.take(scattered, prefix_owner, axis=0)
    wanted = lax.all_to_all(
        jnp.broadcast_to(request_prefix[None], (req_count, requests)), "req", 0, 0, tiled=True
    )
    outgoing = jnp.take(owner_pieces, wanted.reshape(-1), axis=0).reshape(
        req_count, requests, piece, 2, width
    )
    arrived = lax.all_to_all(outgoing, "req", 0, 0, tiled=True)
    return jnp.transpose(arrived, (1, 0, 2, 3, 4)).reshape(requests, plen, 2, width)


def tp_reduce_scatter(values, tp_count):
    rows, width = values.shape
    share = width // tp_count
    chunks = jnp.transpose(
        values.astype(jnp.bfloat16).reshape(rows, tp_count, share), (1, 0, 2)
    )
    arrived = lax.all_to_all(chunks, "tp", 0, 0, tiled=True)
    return arrived.astype(jnp.float32).sum(axis=0)


def tp_all_gather(share_values, tp_count):
    rows, share = share_values.shape
    copies = jnp.broadcast_to(share_values[None], (tp_count, rows, share))
    arrived = lax.all_to_all(copies, "tp", 0, 0, tiled=True)
    return jnp.transpose(arrived, (1, 0, 2)).reshape(rows, tp_count * share)


def attend_local(queries, suffix_kv, chosen, suffix_len, requests, slot_len):
    kv_local = suffix_kv.shape[2] // HD
    group_size = HEADS // KVH
    plen_local = chosen.shape[1]
    query_block = queries.reshape(requests, slot_len, kv_local, group_size, HD)
    cache_block = chosen.reshape(requests, plen_local, 2, kv_local, HD)
    suffix_block = suffix_kv.reshape(requests, slot_len, 2, kv_local, HD)
    score_scale = 1.0 / math.sqrt(HD)
    prefix_score = (
        jnp.einsum(
            "rikgd,rjkd->rkgij",
            query_block,
            cache_block[:, :, 0],
            preferred_element_type=jnp.float32,
        )
        * score_scale
    )
    suffix_score = (
        jnp.einsum(
            "rikgd,rjkd->rkgij",
            query_block,
            suffix_block[:, :, 0],
            preferred_element_type=jnp.float32,
        )
        * score_scale
    )
    positions = jnp.arange(slot_len, dtype=jnp.int32)
    allowed = (positions[None, None, :] <= positions[None, :, None]) & (
        positions[None, None, :] < suffix_len[:, None, None]
    )
    suffix_score = jnp.where(allowed[:, None, None], suffix_score, -1e30)
    score_peak = jnp.maximum(prefix_score.max(-1), suffix_score.max(-1))[..., None]
    prefix_exp = jnp.exp(prefix_score - score_peak)
    suffix_exp = jnp.exp(suffix_score - score_peak)
    normaliser = prefix_exp.sum(-1, keepdims=True) + suffix_exp.sum(-1, keepdims=True)
    prefix_prob = (prefix_exp / normaliser).astype(jnp.bfloat16)
    suffix_prob = (suffix_exp / normaliser).astype(jnp.bfloat16)
    mixed_values = jnp.einsum(
        "rkgij,rjkd->rikgd", prefix_prob, cache_block[:, :, 1], preferred_element_type=jnp.float32
    )
    mixed_values = mixed_values + jnp.einsum(
        "rkgij,rjkd->rikgd", suffix_prob, suffix_block[:, :, 1], preferred_element_type=jnp.float32
    )
    return mixed_values.reshape(requests * slot_len, kv_local * group_size * HD).astype(
        jnp.bfloat16
    )


def routing_tables(routes, live_rows, route_weight):
    expert_ids = jnp.arange(EXPERTS, dtype=jnp.int32)
    member = (routes[:, :, None] == expert_ids) & live_rows[:, None, None]
    member_int = member.astype(jnp.int32)
    flat_member = member_int.reshape(-1, EXPERTS)
    earlier = jnp.cumsum(flat_member, axis=0) - flat_member
    slot_index = jnp.sum(earlier * flat_member, axis=1).reshape(routes.shape)
    slot_hit = (slot_index[:, :, None] == jnp.arange(CAP, dtype=jnp.int32)).astype(jnp.float32)
    member_float = member.astype(jnp.float32)
    placing = (
        jnp.einsum("tke,tkc->ect", member_float, slot_hit)
        .reshape(EXPERTS * CAP, routes.shape[0])
        .astype(jnp.bfloat16)
    )
    combining = jnp.einsum(
        "tke,tkc,tk->tec", member_float, slot_hit, route_weight, precision=lax.Precision.HIGHEST
    )
    return (placing, combining.reshape(routes.shape[0], EXPERTS * CAP))


def expert_apply(arrived, w_gate, w_up, w_down):
    flat_rows = arrived.reshape(-1, w_gate.shape[1])
    gate_value = jnp.dot(flat_rows, w_gate[0], preferred_element_type=jnp.float32)
    up_value = jnp.dot(flat_rows, w_up[0], preferred_element_type=jnp.float32)
    hidden_units = (jax.nn.silu(gate_value) * up_value).astype(jnp.bfloat16)
    piece_out = jnp.dot(hidden_units, w_down[0], preferred_element_type=jnp.float32).astype(
        jnp.bfloat16
    )
    return piece_out.reshape(arrived.shape)


def send_back(parts):
    return lax.all_to_all(parts, "req", split_axis=0, concat_axis=0, tiled=True)


def per_device(
    queries,
    suffix_kv,
    prefix_cache,
    prefix_owner,
    request_prefix,
    suffix_len,
    residual,
    norm_gain,
    router,
    routes,
    w_gate,
    w_up,
    w_down,
    w_out,
):
    tp_count = lax.axis_size("tp")
    tp_index = lax.axis_index("tp")
    req_count = lax.axis_size("req")
    model_width = residual.shape[1]
    share_width = model_width // tp_count
    share_start = tp_index * share_width
    requests = request_prefix.shape[0]
    slot_len = queries.shape[0] // requests
    chosen = fetch_prefixes(prefix_cache, prefix_owner, request_prefix, req_count)
    attended = attend_local(queries, suffix_kv, chosen, suffix_len, requests, slot_len)
    partial_value = jnp.dot(attended, w_out, preferred_element_type=jnp.float32)
    attn_share = tp_reduce_scatter(partial_value, tp_count)
    attn_full = tp_all_gather(attn_share.astype(jnp.bfloat16), tp_count)
    hidden_state = residual.astype(jnp.float32) + attn_full.astype(jnp.float32)
    residual_share = lax.dynamic_slice_in_dim(residual, share_start, share_width, 1)
    hidden_share = residual_share.astype(jnp.float32) + attn_share
    inverse = lax.rsqrt(jnp.mean(hidden_state * hidden_state, axis=1, keepdims=True) + 1e-05)
    scaled = hidden_state * norm_gain * inverse
    logits = jnp.dot(scaled, router, precision=lax.Precision.HIGHEST)
    normed_full = scaled.astype(jnp.bfloat16)
    route_hit = (routes[:, :, None] == jnp.arange(EXPERTS, dtype=jnp.int32)).astype(jnp.float32)
    picked_logit = jnp.sum(route_hit * logits[:, None, :], axis=2)
    first_weight = jax.nn.sigmoid(picked_logit[:, 0] - picked_logit[:, 1])
    route_weight = jnp.stack([first_weight, 1.0 - first_weight], axis=1)
    live_rows = jnp.arange(routes.shape[0], dtype=jnp.int32) % slot_len < jnp.repeat(
        suffix_len, slot_len
    )
    placing, combining = routing_tables(routes, live_rows, route_weight)
    repeats = req_count // EXPERTS
    tokens = routes.shape[0]
    chunk_slots = CAP // CHUNKS
    packed_rows = chunk_slots * model_width // LANES
    placing_blocks = placing.reshape(EXPERTS, CAP, tokens)
    combining_blocks = combining.reshape(tokens, EXPERTS, CAP)
    share_rows = chunk_slots * share_width // LANES
    mixture_share = jnp.zeros((tokens, share_width), jnp.float32)
    for chunk in range(CHUNKS):
        slots = slice(chunk * chunk_slots, (chunk + 1) * chunk_slots)
        chunk_placing = placing_blocks[:, slots].reshape(EXPERTS * chunk_slots, tokens)
        send_rows = jnp.dot(chunk_placing, normed_full, preferred_element_type=jnp.float32).astype(
            jnp.bfloat16
        )
        outgoing = jnp.tile(send_rows.reshape(EXPERTS, packed_rows, LANES), (repeats, 1, 1))
        arrived = lax.all_to_all(outgoing, "req", split_axis=0, concat_axis=0, tiled=True)
        piece_out = expert_apply(arrived, w_gate, w_up, w_down).reshape(-1, model_width)
        reduced = lax.psum_scatter(piece_out, "tp", scatter_dimension=1, tiled=True)
        returned = send_back(reduced.reshape(req_count, share_rows, LANES))
        summed = returned.astype(jnp.float32).reshape(repeats, EXPERTS, share_rows, LANES).sum(
            axis=0
        )
        mixture_share = mixture_share + jnp.dot(
            combining_blocks[:, :, slots].reshape(tokens, EXPERTS * chunk_slots),
            summed.reshape(EXPERTS * chunk_slots, share_width),
            precision=lax.Precision.HIGHEST,
        )
    layer_out = jnp.where(live_rows[:, None], hidden_share + mixture_share, 0.0)
    return layer_out.astype(jnp.bfloat16)


def solution(mesh):
    return jax.shard_map(
        per_device,
        mesh=mesh,
        in_specs=(
            P("req", "tp"),
            P("req", None, "tp"),
            P("req", None, None, "tp"),
            P(),
            P("req"),
            P("req"),
            P("req", None),
            P(),
            P(),
            P("req", None),
            P("req", None, "tp"),
            P("req", None, "tp"),
            P("req", "tp", None),
            P("tp", None),
        ),
        out_specs=P("req", "tp"),
        check_vma=False,
    )
```

```python
import math

import jax
import jax.numpy as jnp
from jax import lax
from jax.sharding import PartitionSpec as P

HEADS = 32
KVH = 8
HD = 128
EXPERTS = 8
NPFX = 4
CAP = 18
LANES = 128
CHUNKS = 3


def broadcast(x, axis, root):
    mine = lax.axis_index(axis) == root
    return lax.psum(jnp.where(mine, x, jnp.zeros_like(x)), axis)


def fetch_prefixes(prefix_cache, prefix_owner, request_prefix, req_count):
    plen = prefix_cache.shape[1]
    width = prefix_cache.shape[3]
    piece = plen // req_count
    requests = request_prefix.shape[0]
    pieces = prefix_cache.reshape(req_count, piece, 2, width)
    scattered = lax.all_to_all(pieces, "req", 0, 0, tiled=True)
    owner_pieces = jnp.take(scattered, prefix_owner, axis=0)
    wanted = lax.all_gather(request_prefix, "req", tiled=True)
    outgoing = jnp.take(owner_pieces, wanted.reshape(-1), axis=0).reshape(
        req_count, requests, piece, 2, width
    )
    arrived = lax.all_to_all(outgoing, "req", 0, 0, tiled=True)
    return jnp.transpose(arrived, (1, 0, 2, 3, 4)).reshape(requests, plen, 2, width)


def tp_reduce_scatter(values, tp_count):
    rows, width = values.shape
    share = width // tp_count
    chunks = jnp.transpose(
        values.astype(jnp.bfloat16).reshape(rows, tp_count, share), (1, 0, 2)
    )
    arrived = lax.all_to_all(chunks, "tp", 0, 0, tiled=True)
    return arrived.astype(jnp.float32).sum(axis=0)


def tp_all_gather(share_values, tp_count):
    rows, share = share_values.shape
    copies = jnp.broadcast_to(share_values[None], (tp_count, rows, share))
    arrived = lax.all_to_all(copies, "tp", 0, 0, tiled=True)
    return jnp.transpose(arrived, (1, 0, 2)).reshape(rows, tp_count * share)


def attend_local(queries, suffix_kv, chosen, suffix_len, requests, slot_len):
    kv_local = suffix_kv.shape[2] // HD
    group_size = HEADS // KVH
    plen_local = chosen.shape[1]
    query_block = queries.reshape(requests, slot_len, kv_local, group_size, HD)
    cache_block = chosen.reshape(requests, plen_local, 2, kv_local, HD)
    suffix_block = suffix_kv.reshape(requests, slot_len, 2, kv_local, HD)
    score_scale = 1.0 / math.sqrt(HD)
    prefix_score = (
        jnp.einsum(
            "rikgd,rjkd->rkgij",
            query_block,
            cache_block[:, :, 0],
            preferred_element_type=jnp.float32,
        )
        * score_scale
    )
    suffix_score = (
        jnp.einsum(
            "rikgd,rjkd->rkgij",
            query_block,
            suffix_block[:, :, 0],
            preferred_element_type=jnp.float32,
        )
        * score_scale
    )
    positions = jnp.arange(slot_len, dtype=jnp.int32)
    allowed = (positions[None, None, :] <= positions[None, :, None]) & (
        positions[None, None, :] < suffix_len[:, None, None]
    )
    suffix_score = jnp.where(allowed[:, None, None], suffix_score, -1e30)
    score_peak = jnp.maximum(prefix_score.max(-1), suffix_score.max(-1))[..., None]
    prefix_exp = jnp.exp(prefix_score - score_peak)
    suffix_exp = jnp.exp(suffix_score - score_peak)
    normaliser = prefix_exp.sum(-1, keepdims=True) + suffix_exp.sum(-1, keepdims=True)
    prefix_prob = (prefix_exp / normaliser).astype(jnp.bfloat16)
    suffix_prob = (suffix_exp / normaliser).astype(jnp.bfloat16)
    mixed_values = jnp.einsum(
        "rkgij,rjkd->rikgd", prefix_prob, cache_block[:, :, 1], preferred_element_type=jnp.float32
    )
    mixed_values = mixed_values + jnp.einsum(
        "rkgij,rjkd->rikgd", suffix_prob, suffix_block[:, :, 1], preferred_element_type=jnp.float32
    )
    return mixed_values.reshape(requests * slot_len, kv_local * group_size * HD).astype(
        jnp.bfloat16
    )


def routing_tables(routes, live_rows, route_weight):
    expert_ids = jnp.arange(EXPERTS, dtype=jnp.int32)
    member = (routes[:, :, None] == expert_ids) & live_rows[:, None, None]
    member_int = member.astype(jnp.int32)
    flat_member = member_int.reshape(-1, EXPERTS)
    earlier = jnp.cumsum(flat_member, axis=0) - flat_member
    slot_index = jnp.sum(earlier * flat_member, axis=1).reshape(routes.shape)
    slot_hit = (slot_index[:, :, None] == jnp.arange(CAP, dtype=jnp.int32)).astype(jnp.float32)
    member_float = member.astype(jnp.float32)
    placing = (
        jnp.einsum("tke,tkc->ect", member_float, slot_hit)
        .reshape(EXPERTS * CAP, routes.shape[0])
        .astype(jnp.bfloat16)
    )
    combining = jnp.einsum(
        "tke,tkc,tk->tec", member_float, slot_hit, route_weight, precision=lax.Precision.HIGHEST
    )
    return (placing, combining.reshape(routes.shape[0], EXPERTS * CAP))


def expert_apply(arrived, w_gate, w_up, w_down):
    flat_rows = arrived.reshape(-1, w_gate.shape[1])
    gate_value = jnp.dot(flat_rows, w_gate[0], preferred_element_type=jnp.float32)
    up_value = jnp.dot(flat_rows, w_up[0], preferred_element_type=jnp.float32)
    hidden_units = (jax.nn.silu(gate_value) * up_value).astype(jnp.bfloat16)
    piece_out = jnp.dot(hidden_units, w_down[0], preferred_element_type=jnp.float32).astype(
        jnp.bfloat16
    )
    return piece_out.reshape(arrived.shape)


def send_back(parts):
    return lax.all_to_all(parts, "req", split_axis=0, concat_axis=0, tiled=True)


def per_device(
    queries,
    suffix_kv,
    prefix_cache,
    prefix_owner,
    request_prefix,
    suffix_len,
    residual,
    norm_gain,
    router,
    routes,
    w_gate,
    w_up,
    w_down,
    w_out,
):
    tp_count = lax.axis_size("tp")
    tp_index = lax.axis_index("tp")
    req_count = lax.axis_size("req")
    model_width = residual.shape[1]
    share_width = model_width // tp_count
    share_start = tp_index * share_width
    requests = request_prefix.shape[0]
    slot_len = queries.shape[0] // requests
    chosen = fetch_prefixes(prefix_cache, prefix_owner, request_prefix, req_count)
    attended = attend_local(queries, suffix_kv, chosen, suffix_len, requests, slot_len)
    partial_value = jnp.dot(attended, w_out, preferred_element_type=jnp.float32)
    attn_share = tp_reduce_scatter(partial_value, tp_count)
    attn_full = tp_all_gather(attn_share.astype(jnp.bfloat16), tp_count)
    hidden_state = residual.astype(jnp.float32) + attn_full.astype(jnp.float32)
    residual_share = lax.dynamic_slice_in_dim(residual, share_start, share_width, 1)
    hidden_share = residual_share.astype(jnp.float32) + attn_share
    inverse = lax.rsqrt(jnp.mean(hidden_state * hidden_state, axis=1, keepdims=True) + 1e-05)
    scaled = hidden_state * norm_gain * inverse
    logits = jnp.dot(scaled, router, precision=lax.Precision.HIGHEST)
    normed_full = scaled.astype(jnp.bfloat16)
    route_hit = (routes[:, :, None] == jnp.arange(EXPERTS, dtype=jnp.int32)).astype(jnp.float32)
    picked_logit = jnp.sum(route_hit * logits[:, None, :], axis=2)
    first_weight = jax.nn.sigmoid(picked_logit[:, 0] - picked_logit[:, 1])
    route_weight = jnp.stack([first_weight, 1.0 - first_weight], axis=1)
    live_rows = jnp.arange(routes.shape[0], dtype=jnp.int32) % slot_len < jnp.repeat(
        suffix_len, slot_len
    )
    placing, combining = routing_tables(routes, live_rows, route_weight)
    repeats = req_count // EXPERTS
    tokens = routes.shape[0]
    chunk_slots = CAP // CHUNKS
    packed_rows = chunk_slots * model_width // LANES
    placing_blocks = placing.reshape(EXPERTS, CAP, tokens)
    combining_blocks = combining.reshape(tokens, EXPERTS, CAP)
    share_rows = chunk_slots * share_width // LANES
    mixture_share = jnp.zeros((tokens, share_width), jnp.float32)
    for chunk in range(CHUNKS):
        slots = slice(chunk * chunk_slots, (chunk + 1) * chunk_slots)
        chunk_placing = placing_blocks[:, slots].reshape(EXPERTS * chunk_slots, tokens)
        send_rows = jnp.dot(chunk_placing, normed_full, preferred_element_type=jnp.float32).astype(
            jnp.bfloat16
        )
        outgoing = jnp.tile(send_rows.reshape(EXPERTS, packed_rows, LANES), (repeats, 1, 1))
        arrived = lax.all_to_all(outgoing, "req", split_axis=0, concat_axis=0, tiled=True)
        piece_out = expert_apply(arrived, w_gate, w_up, w_down).reshape(-1, model_width)
        reduced = lax.psum_scatter(piece_out, "tp", scatter_dimension=1, tiled=True)
        returned = send_back(reduced.reshape(req_count, share_rows, LANES))
        summed = returned.astype(jnp.float32).reshape(repeats, EXPERTS, share_rows, LANES).sum(
            axis=0
        )
        mixture_share = mixture_share + jnp.dot(
            combining_blocks[:, :, slots].reshape(tokens, EXPERTS * chunk_slots),
            summed.reshape(EXPERTS * chunk_slots, share_width),
            precision=lax.Precision.HIGHEST,
        )
    layer_out = jnp.where(live_rows[:, None], hidden_share + mixture_share, 0.0)
    return layer_out.astype(jnp.bfloat16)


def solution(mesh):
    return jax.shard_map(
        per_device,
        mesh=mesh,
        in_specs=(
            P("req", "tp"),
            P("req", None, "tp"),
            P("req", None, None, "tp"),
            P(),
            P("req"),
            P("req"),
            P("req", None),
            P(),
            P(),
            P("req", None),
            P("req", None, "tp"),
            P("req", None, "tp"),
            P("req", "tp", None),
            P("tp", None),
        ),
        out_specs=P("req", "tp"),
        check_vma=False,
    )
```

```python
import math

import jax
import jax.numpy as jnp
from jax import lax
from jax.sharding import PartitionSpec as P

HEADS = 32
KVH = 8
HD = 128
EXPERTS = 8
NPFX = 4
CAP = 18
LANES = 128
CHUNKS = 2


def broadcast(x, axis, root):
    mine = lax.axis_index(axis) == root
    return lax.psum(jnp.where(mine, x, jnp.zeros_like(x)), axis)


def fetch_prefixes(prefix_cache, prefix_owner, request_prefix, req_count):
    plen = prefix_cache.shape[1]
    width = prefix_cache.shape[3]
    piece = plen // req_count
    requests = request_prefix.shape[0]
    pieces = prefix_cache.reshape(req_count, piece, 2, width)
    tag_rows = 16
    tags = jnp.zeros((tag_rows, 2, width), jnp.bfloat16)
    tags = tags.at[0, 0, :requests].set(request_prefix.astype(jnp.bfloat16))
    tagged = jnp.concatenate(
        [pieces, jnp.broadcast_to(tags[None], (req_count, tag_rows, 2, width))], axis=1
    )
    scattered = lax.all_to_all(tagged, "req", 0, 0, tiled=True)
    owner_pieces = jnp.take(scattered[:, :piece], prefix_owner, axis=0)
    wanted = scattered[:, piece, 0, :requests].astype(jnp.int32)
    outgoing = jnp.take(owner_pieces, wanted.reshape(-1), axis=0).reshape(
        req_count, requests, piece, 2, width
    )
    arrived = lax.all_to_all(outgoing, "req", 0, 0, tiled=True)
    return jnp.transpose(arrived, (1, 0, 2, 3, 4)).reshape(requests, plen, 2, width)


def tp_reduce_scatter(values, tp_count):
    rows, width = values.shape
    share = width // tp_count
    chunks = jnp.transpose(
        values.astype(jnp.bfloat16).reshape(rows, tp_count, share), (1, 0, 2)
    )
    arrived = lax.all_to_all(chunks, "tp", 0, 0, tiled=True)
    return arrived.astype(jnp.float32).sum(axis=0)


def tp_all_gather(share_values, tp_count):
    rows, share = share_values.shape
    copies = jnp.broadcast_to(share_values[None], (tp_count, rows, share))
    arrived = lax.all_to_all(copies, "tp", 0, 0, tiled=True)
    return jnp.transpose(arrived, (1, 0, 2)).reshape(rows, tp_count * share)


def attend_local(queries, suffix_kv, chosen, suffix_len, requests, slot_len):
    kv_local = suffix_kv.shape[2] // HD
    group_size = HEADS // KVH
    plen_local = chosen.shape[1]
    query_block = queries.reshape(requests, slot_len, kv_local, group_size, HD)
    cache_block = chosen.reshape(requests, plen_local, 2, kv_local, HD)
    suffix_block = suffix_kv.reshape(requests, slot_len, 2, kv_local, HD)
    score_scale = 1.0 / math.sqrt(HD)
    prefix_score = (
        jnp.einsum(
            "rikgd,rjkd->rkgij",
            query_block,
            cache_block[:, :, 0],
            preferred_element_type=jnp.float32,
        )
        * score_scale
    )
    suffix_score = (
        jnp.einsum(
            "rikgd,rjkd->rkgij",
            query_block,
            suffix_block[:, :, 0],
            preferred_element_type=jnp.float32,
        )
        * score_scale
    )
    positions = jnp.arange(slot_len, dtype=jnp.int32)
    allowed = (positions[None, None, :] <= positions[None, :, None]) & (
        positions[None, None, :] < suffix_len[:, None, None]
    )
    suffix_score = jnp.where(allowed[:, None, None], suffix_score, -1e30)
    score_peak = jnp.maximum(prefix_score.max(-1), suffix_score.max(-1))[..., None]
    prefix_exp = jnp.exp(prefix_score - score_peak)
    suffix_exp = jnp.exp(suffix_score - score_peak)
    normaliser = prefix_exp.sum(-1, keepdims=True) + suffix_exp.sum(-1, keepdims=True)
    prefix_prob = (prefix_exp / normaliser).astype(jnp.bfloat16)
    suffix_prob = (suffix_exp / normaliser).astype(jnp.bfloat16)
    mixed_values = jnp.einsum(
        "rkgij,rjkd->rikgd", prefix_prob, cache_block[:, :, 1], preferred_element_type=jnp.float32
    )
    mixed_values = mixed_values + jnp.einsum(
        "rkgij,rjkd->rikgd", suffix_prob, suffix_block[:, :, 1], preferred_element_type=jnp.float32
    )
    return mixed_values.reshape(requests * slot_len, kv_local * group_size * HD).astype(
        jnp.bfloat16
    )


def routing_tables(routes, live_rows, route_weight):
    expert_ids = jnp.arange(EXPERTS, dtype=jnp.int32)
    member = (routes[:, :, None] == expert_ids) & live_rows[:, None, None]
    member_int = member.astype(jnp.int32)
    flat_member = member_int.reshape(-1, EXPERTS)
    earlier = jnp.cumsum(flat_member, axis=0) - flat_member
    slot_index = jnp.sum(earlier * flat_member, axis=1).reshape(routes.shape)
    slot_hit = (slot_index[:, :, None] == jnp.arange(CAP, dtype=jnp.int32)).astype(jnp.float32)
    member_float = member.astype(jnp.float32)
    placing = (
        jnp.einsum("tke,tkc->ect", member_float, slot_hit)
        .reshape(EXPERTS * CAP, routes.shape[0])
        .astype(jnp.bfloat16)
    )
    combining = jnp.einsum(
        "tke,tkc,tk->tec", member_float, slot_hit, route_weight, precision=lax.Precision.HIGHEST
    )
    return (placing, combining.reshape(routes.shape[0], EXPERTS * CAP))


def expert_apply(arrived, w_gate, w_up, w_down):
    flat_rows = arrived.reshape(-1, w_gate.shape[1])
    gate_value = jnp.dot(flat_rows, w_gate[0], preferred_element_type=jnp.float32)
    up_value = jnp.dot(flat_rows, w_up[0], preferred_element_type=jnp.float32)
    hidden_units = (jax.nn.silu(gate_value) * up_value).astype(jnp.bfloat16)
    piece_out = jnp.dot(hidden_units, w_down[0], preferred_element_type=jnp.float32).astype(
        jnp.bfloat16
    )
    return piece_out.reshape(arrived.shape)


def send_back(parts):
    return lax.all_to_all(parts, "req", split_axis=0, concat_axis=0, tiled=True)


def per_device(
    queries,
    suffix_kv,
    prefix_cache,
    prefix_owner,
    request_prefix,
    suffix_len,
    residual,
    norm_gain,
    router,
    routes,
    w_gate,
    w_up,
    w_down,
    w_out,
):
    tp_count = lax.axis_size("tp")
    tp_index = lax.axis_index("tp")
    req_count = lax.axis_size("req")
    model_width = residual.shape[1]
    share_width = model_width // tp_count
    share_start = tp_index * share_width
    requests = request_prefix.shape[0]
    slot_len = queries.shape[0] // requests
    chosen = fetch_prefixes(prefix_cache, prefix_owner, request_prefix, req_count)
    attended = attend_local(queries, suffix_kv, chosen, suffix_len, requests, slot_len)
    partial_value = jnp.dot(attended, w_out, preferred_element_type=jnp.float32)
    attn_share = tp_reduce_scatter(partial_value, tp_count)
    attn_full = tp_all_gather(attn_share.astype(jnp.bfloat16), tp_count)
    hidden_state = residual.astype(jnp.float32) + attn_full.astype(jnp.float32)
    residual_share = lax.dynamic_slice_in_dim(residual, share_start, share_width, 1)
    hidden_share = residual_share.astype(jnp.float32) + attn_share
    inverse = lax.rsqrt(jnp.mean(hidden_state * hidden_state, axis=1, keepdims=True) + 1e-05)
    scaled = hidden_state * norm_gain * inverse
    logits = jnp.dot(scaled, router, precision=lax.Precision.HIGHEST)
    normed_full = scaled.astype(jnp.bfloat16)
    route_hit = (routes[:, :, None] == jnp.arange(EXPERTS, dtype=jnp.int32)).astype(jnp.float32)
    picked_logit = jnp.sum(route_hit * logits[:, None, :], axis=2)
    first_weight = jax.nn.sigmoid(picked_logit[:, 0] - picked_logit[:, 1])
    route_weight = jnp.stack([first_weight, 1.0 - first_weight], axis=1)
    live_rows = jnp.arange(routes.shape[0], dtype=jnp.int32) % slot_len < jnp.repeat(
        suffix_len, slot_len
    )
    placing, combining = routing_tables(routes, live_rows, route_weight)
    repeats = req_count // EXPERTS
    tokens = routes.shape[0]
    chunk_slots = CAP // CHUNKS
    packed_rows = chunk_slots * model_width // LANES
    placing_blocks = placing.reshape(EXPERTS, CAP, tokens)
    combining_blocks = combining.reshape(tokens, EXPERTS, CAP)
    share_rows = chunk_slots * share_width // LANES
    mixture_share = jnp.zeros((tokens, share_width), jnp.float32)
    for chunk in range(CHUNKS):
        slots = slice(chunk * chunk_slots, (chunk + 1) * chunk_slots)
        chunk_placing = placing_blocks[:, slots].reshape(EXPERTS * chunk_slots, tokens)
        send_rows = jnp.dot(chunk_placing, normed_full, preferred_element_type=jnp.float32).astype(
            jnp.bfloat16
        )
        outgoing = jnp.tile(send_rows.reshape(EXPERTS, packed_rows, LANES), (repeats, 1, 1))
        arrived = lax.all_to_all(outgoing, "req", split_axis=0, concat_axis=0, tiled=True)
        piece_out = expert_apply(arrived, w_gate, w_up, w_down).reshape(-1, model_width)
        reduced = lax.psum_scatter(piece_out, "tp", scatter_dimension=1, tiled=True)
        returned = send_back(reduced.reshape(req_count, share_rows, LANES))
        summed = returned.astype(jnp.float32).reshape(repeats, EXPERTS, share_rows, LANES).sum(
            axis=0
        )
        mixture_share = mixture_share + jnp.dot(
            combining_blocks[:, :, slots].reshape(tokens, EXPERTS * chunk_slots),
            summed.reshape(EXPERTS * chunk_slots, share_width),
            precision=lax.Precision.HIGHEST,
        )
    layer_out = jnp.where(live_rows[:, None], hidden_share + mixture_share, 0.0)
    return layer_out.astype(jnp.bfloat16)


def solution(mesh):
    return jax.shard_map(
        per_device,
        mesh=mesh,
        in_specs=(
            P("req", "tp"),
            P("req", None, "tp"),
            P("req", None, None, "tp"),
            P(),
            P("req"),
            P("req"),
            P("req", None),
            P(),
            P(),
            P("req", None),
            P("req", None, "tp"),
            P("req", None, "tp"),
            P("req", "tp", None),
            P("tp", None),
        ),
        out_specs=P("req", "tp"),
        check_vma=False,
    )
```

```python
import math

import jax
import jax.numpy as jnp
from jax import lax
from jax.sharding import PartitionSpec as P

HEADS = 32
KVH = 8
HD = 128
EXPERTS = 8
NPFX = 4
CAP = 18
LANES = 128
CHUNKS = 2


def broadcast(x, axis, root):
    mine = lax.axis_index(axis) == root
    return lax.psum(jnp.where(mine, x, jnp.zeros_like(x)), axis)


def fetch_prefixes(prefix_cache, prefix_owner, request_prefix, req_count):
    plen = prefix_cache.shape[1]
    width = prefix_cache.shape[3]
    piece = plen // req_count
    requests = request_prefix.shape[0]
    pieces = prefix_cache.reshape(req_count, piece, 2, width)
    tag_rows = 16
    tags = jnp.zeros((tag_rows, 2, width), jnp.bfloat16)
    tags = tags.at[0, 0, :requests].set(request_prefix.astype(jnp.bfloat16))
    tagged = jnp.concatenate(
        [pieces, jnp.broadcast_to(tags[None], (req_count, tag_rows, 2, width))], axis=1
    )
    scattered = lax.all_to_all(tagged, "req", 0, 0, tiled=True)
    owner_pieces = jnp.take(scattered[:, :piece], prefix_owner, axis=0)
    wanted = scattered[:, piece, 0, :requests].astype(jnp.int32)
    outgoing = jnp.take(owner_pieces, wanted.reshape(-1), axis=0).reshape(
        req_count, requests, piece, 2, width
    )
    arrived = lax.all_to_all(outgoing, "req", 0, 0, tiled=True)
    return jnp.transpose(arrived, (1, 0, 2, 3, 4)).reshape(requests, plen, 2, width)


def tp_reduce_scatter(values, tp_count):
    rows, width = values.shape
    share = width // tp_count
    me = lax.axis_index("tp")
    chunks = values.astype(jnp.bfloat16).reshape(rows, tp_count, share)
    total = lax.dynamic_index_in_dim(chunks, me, axis=1, keepdims=False).astype(jnp.float32)
    for shift in range(1, tp_count):
        outgoing = lax.dynamic_index_in_dim(chunks, (me + shift) % tp_count, axis=1, keepdims=False)
        pairs = [(i, (i + shift) % tp_count) for i in range(tp_count)]
        total = total + lax.ppermute(outgoing, "tp", pairs).astype(jnp.float32)
    return total


def tp_all_gather(share_values, tp_count):
    rows, share = share_values.shape
    me = lax.axis_index("tp")
    gathered = jnp.zeros((rows, tp_count, share), share_values.dtype)
    gathered = lax.dynamic_update_index_in_dim(gathered, share_values, me, axis=1)
    for shift in range(1, tp_count):
        pairs = [(i, (i + shift) % tp_count) for i in range(tp_count)]
        arrived = lax.ppermute(share_values, "tp", pairs)
        gathered = lax.dynamic_update_index_in_dim(
            gathered, arrived, (me - shift) % tp_count, axis=1
        )
    return gathered.reshape(rows, tp_count * share)


def attend_local(queries, suffix_kv, chosen, suffix_len, requests, slot_len):
    kv_local = suffix_kv.shape[2] // HD
    group_size = HEADS // KVH
    plen_local = chosen.shape[1]
    query_block = queries.reshape(requests, slot_len, kv_local, group_size, HD)
    cache_block = chosen.reshape(requests, plen_local, 2, kv_local, HD)
    suffix_block = suffix_kv.reshape(requests, slot_len, 2, kv_local, HD)
    score_scale = 1.0 / math.sqrt(HD)
    prefix_score = (
        jnp.einsum(
            "rikgd,rjkd->rkgij",
            query_block,
            cache_block[:, :, 0],
            preferred_element_type=jnp.float32,
        )
        * score_scale
    )
    suffix_score = (
        jnp.einsum(
            "rikgd,rjkd->rkgij",
            query_block,
            suffix_block[:, :, 0],
            preferred_element_type=jnp.float32,
        )
        * score_scale
    )
    positions = jnp.arange(slot_len, dtype=jnp.int32)
    allowed = (positions[None, None, :] <= positions[None, :, None]) & (
        positions[None, None, :] < suffix_len[:, None, None]
    )
    suffix_score = jnp.where(allowed[:, None, None], suffix_score, -1e30)
    score_peak = jnp.maximum(prefix_score.max(-1), suffix_score.max(-1))[..., None]
    prefix_exp = jnp.exp(prefix_score - score_peak)
    suffix_exp = jnp.exp(suffix_score - score_peak)
    normaliser = prefix_exp.sum(-1, keepdims=True) + suffix_exp.sum(-1, keepdims=True)
    prefix_prob = (prefix_exp / normaliser).astype(jnp.bfloat16)
    suffix_prob = (suffix_exp / normaliser).astype(jnp.bfloat16)
    mixed_values = jnp.einsum(
        "rkgij,rjkd->rikgd", prefix_prob, cache_block[:, :, 1], preferred_element_type=jnp.float32
    )
    mixed_values = mixed_values + jnp.einsum(
        "rkgij,rjkd->rikgd", suffix_prob, suffix_block[:, :, 1], preferred_element_type=jnp.float32
    )
    return mixed_values.reshape(requests * slot_len, kv_local * group_size * HD).astype(
        jnp.bfloat16
    )


def routing_tables(routes, live_rows, route_weight):
    expert_ids = jnp.arange(EXPERTS, dtype=jnp.int32)
    member = (routes[:, :, None] == expert_ids) & live_rows[:, None, None]
    member_int = member.astype(jnp.int32)
    flat_member = member_int.reshape(-1, EXPERTS)
    earlier = jnp.cumsum(flat_member, axis=0) - flat_member
    slot_index = jnp.sum(earlier * flat_member, axis=1).reshape(routes.shape)
    slot_hit = (slot_index[:, :, None] == jnp.arange(CAP, dtype=jnp.int32)).astype(jnp.float32)
    member_float = member.astype(jnp.float32)
    placing = (
        jnp.einsum("tke,tkc->ect", member_float, slot_hit)
        .reshape(EXPERTS * CAP, routes.shape[0])
        .astype(jnp.bfloat16)
    )
    combining = jnp.einsum(
        "tke,tkc,tk->tec", member_float, slot_hit, route_weight, precision=lax.Precision.HIGHEST
    )
    return (placing, combining.reshape(routes.shape[0], EXPERTS * CAP))


def expert_apply(arrived, w_gate, w_up, w_down):
    flat_rows = arrived.reshape(-1, w_gate.shape[1])
    gate_value = jnp.dot(flat_rows, w_gate[0], preferred_element_type=jnp.float32)
    up_value = jnp.dot(flat_rows, w_up[0], preferred_element_type=jnp.float32)
    hidden_units = (jax.nn.silu(gate_value) * up_value).astype(jnp.bfloat16)
    piece_out = jnp.dot(hidden_units, w_down[0], preferred_element_type=jnp.float32).astype(
        jnp.bfloat16
    )
    return piece_out.reshape(arrived.shape)


def send_back(parts):
    return lax.all_to_all(parts, "req", split_axis=0, concat_axis=0, tiled=True)


def per_device(
    queries,
    suffix_kv,
    prefix_cache,
    prefix_owner,
    request_prefix,
    suffix_len,
    residual,
    norm_gain,
    router,
    routes,
    w_gate,
    w_up,
    w_down,
    w_out,
):
    tp_count = lax.axis_size("tp")
    tp_index = lax.axis_index("tp")
    req_count = lax.axis_size("req")
    model_width = residual.shape[1]
    share_width = model_width // tp_count
    share_start = tp_index * share_width
    requests = request_prefix.shape[0]
    slot_len = queries.shape[0] // requests
    chosen = fetch_prefixes(prefix_cache, prefix_owner, request_prefix, req_count)
    attended = attend_local(queries, suffix_kv, chosen, suffix_len, requests, slot_len)
    partial_value = jnp.dot(attended, w_out, preferred_element_type=jnp.float32)
    attn_share = tp_reduce_scatter(partial_value, tp_count)
    attn_full = tp_all_gather(attn_share.astype(jnp.bfloat16), tp_count)
    hidden_state = residual.astype(jnp.float32) + attn_full.astype(jnp.float32)
    residual_share = lax.dynamic_slice_in_dim(residual, share_start, share_width, 1)
    hidden_share = residual_share.astype(jnp.float32) + attn_share
    inverse = lax.rsqrt(jnp.mean(hidden_state * hidden_state, axis=1, keepdims=True) + 1e-05)
    scaled = hidden_state * norm_gain * inverse
    logits = jnp.dot(scaled, router, precision=lax.Precision.HIGHEST)
    normed_full = scaled.astype(jnp.bfloat16)
    route_hit = (routes[:, :, None] == jnp.arange(EXPERTS, dtype=jnp.int32)).astype(jnp.float32)
    picked_logit = jnp.sum(route_hit * logits[:, None, :], axis=2)
    first_weight = jax.nn.sigmoid(picked_logit[:, 0] - picked_logit[:, 1])
    route_weight = jnp.stack([first_weight, 1.0 - first_weight], axis=1)
    live_rows = jnp.arange(routes.shape[0], dtype=jnp.int32) % slot_len < jnp.repeat(
        suffix_len, slot_len
    )
    placing, combining = routing_tables(routes, live_rows, route_weight)
    repeats = req_count // EXPERTS
    tokens = routes.shape[0]
    chunk_slots = CAP // CHUNKS
    packed_rows = chunk_slots * model_width // LANES
    placing_blocks = placing.reshape(EXPERTS, CAP, tokens)
    combining_blocks = combining.reshape(tokens, EXPERTS, CAP)
    share_rows = chunk_slots * share_width // LANES
    mixture_share = jnp.zeros((tokens, share_width), jnp.float32)
    for chunk in range(CHUNKS):
        slots = slice(chunk * chunk_slots, (chunk + 1) * chunk_slots)
        chunk_placing = placing_blocks[:, slots].reshape(EXPERTS * chunk_slots, tokens)
        send_rows = jnp.dot(chunk_placing, normed_full, preferred_element_type=jnp.float32).astype(
            jnp.bfloat16
        )
        outgoing = jnp.tile(send_rows.reshape(EXPERTS, packed_rows, LANES), (repeats, 1, 1))
        arrived = lax.all_to_all(outgoing, "req", split_axis=0, concat_axis=0, tiled=True)
        piece_out = expert_apply(arrived, w_gate, w_up, w_down).reshape(-1, model_width)
        reduced = lax.psum_scatter(piece_out, "tp", scatter_dimension=1, tiled=True)
        returned = send_back(reduced.reshape(req_count, share_rows, LANES))
        summed = returned.astype(jnp.float32).reshape(repeats, EXPERTS, share_rows, LANES).sum(
            axis=0
        )
        mixture_share = mixture_share + jnp.dot(
            combining_blocks[:, :, slots].reshape(tokens, EXPERTS * chunk_slots),
            summed.reshape(EXPERTS * chunk_slots, share_width),
            precision=lax.Precision.HIGHEST,
        )
    layer_out = jnp.where(live_rows[:, None], hidden_share + mixture_share, 0.0)
    return layer_out.astype(jnp.bfloat16)


def solution(mesh):
    return jax.shard_map(
        per_device,
        mesh=mesh,
        in_specs=(
            P("req", "tp"),
            P("req", None, "tp"),
            P("req", None, None, "tp"),
            P(),
            P("req"),
            P("req"),
            P("req", None),
            P(),
            P(),
            P("req", None),
            P("req", None, "tp"),
            P("req", None, "tp"),
            P("req", "tp", None),
            P("tp", None),
        ),
        out_specs=P("req", "tp"),
        check_vma=False,
    )
```

```python
import math

import jax
import jax.numpy as jnp
from jax import lax
from jax.sharding import PartitionSpec as P

HEADS = 32
KVH = 8
HD = 128
EXPERTS = 8
NPFX = 4
CAP = 18
LANES = 128
CHUNKS = 2


def broadcast(x, axis, root):
    mine = lax.axis_index(axis) == root
    return lax.psum(jnp.where(mine, x, jnp.zeros_like(x)), axis)


def fetch_prefixes(prefix_cache, prefix_owner, request_prefix, req_count):
    plen = prefix_cache.shape[1]
    width = prefix_cache.shape[3]
    piece = plen // req_count
    requests = request_prefix.shape[0]
    pieces = prefix_cache.reshape(req_count, piece, 2, width)
    tag_rows = 16
    tags = jnp.zeros((tag_rows, 2, width), jnp.bfloat16)
    tags = tags.at[0, 0, :requests].set(request_prefix.astype(jnp.bfloat16))
    tagged = jnp.concatenate(
        [pieces, jnp.broadcast_to(tags[None], (req_count, tag_rows, 2, width))], axis=1
    )
    scattered = lax.all_to_all(tagged, "req", 0, 0, tiled=True)
    owner_pieces = jnp.take(scattered[:, :piece], prefix_owner, axis=0)
    wanted = scattered[:, piece, 0, :requests].astype(jnp.int32)
    outgoing = jnp.take(owner_pieces, wanted.reshape(-1), axis=0).reshape(
        req_count, requests, piece, 2, width
    )
    arrived = lax.all_to_all(outgoing, "req", 0, 0, tiled=True)
    return jnp.transpose(arrived, (1, 0, 2, 3, 4)).reshape(requests, plen, 2, width)


def tp_reduce_scatter(values, tp_count):
    rows, width = values.shape
    share = width // tp_count
    chunks = jnp.transpose(
        values.astype(jnp.bfloat16).reshape(rows, tp_count, share), (1, 0, 2)
    )
    arrived = lax.all_to_all(chunks, "tp", 0, 0, tiled=True)
    return arrived.astype(jnp.float32).sum(axis=0)


def tp_all_gather(share_values, tp_count):
    rows, share = share_values.shape
    copies = jnp.broadcast_to(share_values[None], (tp_count, rows, share))
    arrived = lax.all_to_all(copies, "tp", 0, 0, tiled=True)
    return jnp.transpose(arrived, (1, 0, 2)).reshape(rows, tp_count * share)


def attend_local(queries, suffix_kv, chosen, suffix_len, requests, slot_len):
    kv_local = suffix_kv.shape[2] // HD
    group_size = HEADS // KVH
    plen_local = chosen.shape[1]
    query_block = queries.reshape(requests, slot_len, kv_local, group_size, HD)
    cache_block = chosen.reshape(requests, plen_local, 2, kv_local, HD)
    suffix_block = suffix_kv.reshape(requests, slot_len, 2, kv_local, HD)
    score_scale = 1.0 / math.sqrt(HD)
    prefix_score = (
        jnp.einsum(
            "rikgd,rjkd->rkgij",
            query_block,
            cache_block[:, :, 0],
            preferred_element_type=jnp.float32,
        )
        * score_scale
    )
    suffix_score = (
        jnp.einsum(
            "rikgd,rjkd->rkgij",
            query_block,
            suffix_block[:, :, 0],
            preferred_element_type=jnp.float32,
        )
        * score_scale
    )
    positions = jnp.arange(slot_len, dtype=jnp.int32)
    allowed = (positions[None, None, :] <= positions[None, :, None]) & (
        positions[None, None, :] < suffix_len[:, None, None]
    )
    suffix_score = jnp.where(allowed[:, None, None], suffix_score, -1e30)
    score_peak = jnp.maximum(prefix_score.max(-1), suffix_score.max(-1))[..., None]
    prefix_exp = jnp.exp(prefix_score - score_peak)
    suffix_exp = jnp.exp(suffix_score - score_peak)
    normaliser = prefix_exp.sum(-1, keepdims=True) + suffix_exp.sum(-1, keepdims=True)
    prefix_prob = (prefix_exp / normaliser).astype(jnp.bfloat16)
    suffix_prob = (suffix_exp / normaliser).astype(jnp.bfloat16)
    mixed_values = jnp.einsum(
        "rkgij,rjkd->rikgd", prefix_prob, cache_block[:, :, 1], preferred_element_type=jnp.float32
    )
    mixed_values = mixed_values + jnp.einsum(
        "rkgij,rjkd->rikgd", suffix_prob, suffix_block[:, :, 1], preferred_element_type=jnp.float32
    )
    return mixed_values.reshape(requests * slot_len, kv_local * group_size * HD).astype(
        jnp.bfloat16
    )


def routing_tables(routes, live_rows, route_weight):
    expert_ids = jnp.arange(EXPERTS, dtype=jnp.int32)
    member = (routes[:, :, None] == expert_ids) & live_rows[:, None, None]
    member_int = member.astype(jnp.int32)
    flat_member = member_int.reshape(-1, EXPERTS)
    earlier = jnp.cumsum(flat_member, axis=0) - flat_member
    slot_index = jnp.sum(earlier * flat_member, axis=1).reshape(routes.shape)
    slot_hit = (slot_index[:, :, None] == jnp.arange(CAP, dtype=jnp.int32)).astype(jnp.float32)
    member_float = member.astype(jnp.float32)
    placing = (
        jnp.einsum("tke,tkc->ect", member_float, slot_hit)
        .reshape(EXPERTS * CAP, routes.shape[0])
        .astype(jnp.bfloat16)
    )
    combining = jnp.einsum(
        "tke,tkc,tk->tec", member_float, slot_hit, route_weight, precision=lax.Precision.HIGHEST
    )
    return (placing, combining.reshape(routes.shape[0], EXPERTS * CAP))


def expert_apply(arrived, w_gate, w_up, w_down):
    model_width = w_gate.shape[1]
    blocks = model_width // LANES
    packed = arrived.reshape(-1, blocks, LANES)
    gate_value = jnp.einsum(
        "rkl,klh->rh", packed, w_gate[0].reshape(blocks, LANES, -1),
        preferred_element_type=jnp.float32,
    )
    up_value = jnp.einsum(
        "rkl,klh->rh", packed, w_up[0].reshape(blocks, LANES, -1),
        preferred_element_type=jnp.float32,
    )
    hidden_units = (jax.nn.silu(gate_value) * up_value).astype(jnp.bfloat16)
    piece_out = jnp.dot(hidden_units, w_down[0], preferred_element_type=jnp.float32).astype(
        jnp.bfloat16
    )
    return piece_out.reshape(arrived.shape)


def send_back(parts):
    return lax.all_to_all(parts, "req", split_axis=0, concat_axis=0, tiled=True)


def per_device(
    queries,
    suffix_kv,
    prefix_cache,
    prefix_owner,
    request_prefix,
    suffix_len,
    residual,
    norm_gain,
    router,
    routes,
    w_gate,
    w_up,
    w_down,
    w_out,
):
    tp_count = lax.axis_size("tp")
    tp_index = lax.axis_index("tp")
    req_count = lax.axis_size("req")
    model_width = residual.shape[1]
    share_width = model_width // tp_count
    share_start = tp_index * share_width
    requests = request_prefix.shape[0]
    slot_len = queries.shape[0] // requests
    chosen = fetch_prefixes(prefix_cache, prefix_owner, request_prefix, req_count)
    attended = attend_local(queries, suffix_kv, chosen, suffix_len, requests, slot_len)
    partial_value = jnp.dot(attended, w_out, preferred_element_type=jnp.float32)
    attn_share = tp_reduce_scatter(partial_value, tp_count)
    attn_full = tp_all_gather(attn_share.astype(jnp.bfloat16), tp_count)
    hidden_state = residual.astype(jnp.float32) + attn_full.astype(jnp.float32)
    residual_share = lax.dynamic_slice_in_dim(residual, share_start, share_width, 1)
    hidden_share = residual_share.astype(jnp.float32) + attn_share
    inverse = lax.rsqrt(jnp.mean(hidden_state * hidden_state, axis=1, keepdims=True) + 1e-05)
    scaled = hidden_state * norm_gain * inverse
    logits = jnp.dot(scaled, router, precision=lax.Precision.HIGHEST)
    normed_full = scaled.astype(jnp.bfloat16)
    route_hit = (routes[:, :, None] == jnp.arange(EXPERTS, dtype=jnp.int32)).astype(jnp.float32)
    picked_logit = jnp.sum(route_hit * logits[:, None, :], axis=2)
    first_weight = jax.nn.sigmoid(picked_logit[:, 0] - picked_logit[:, 1])
    route_weight = jnp.stack([first_weight, 1.0 - first_weight], axis=1)
    live_rows = jnp.arange(routes.shape[0], dtype=jnp.int32) % slot_len < jnp.repeat(
        suffix_len, slot_len
    )
    placing, combining = routing_tables(routes, live_rows, route_weight)
    repeats = req_count // EXPERTS
    tokens = routes.shape[0]
    chunk_slots = CAP // CHUNKS
    packed_rows = chunk_slots * model_width // LANES
    placing_blocks = placing.reshape(EXPERTS, CAP, tokens)
    combining_blocks = combining.reshape(tokens, EXPERTS, CAP)
    share_rows = chunk_slots * share_width // LANES
    mixture_share = jnp.zeros((tokens, share_width), jnp.float32)
    for chunk in range(CHUNKS):
        slots = slice(chunk * chunk_slots, (chunk + 1) * chunk_slots)
        chunk_placing = placing_blocks[:, slots].reshape(EXPERTS * chunk_slots, tokens)
        send_rows = jnp.dot(chunk_placing, normed_full, preferred_element_type=jnp.float32).astype(
            jnp.bfloat16
        )
        outgoing = jnp.tile(send_rows.reshape(EXPERTS, packed_rows, LANES), (repeats, 1, 1))
        arrived = lax.all_to_all(outgoing, "req", split_axis=0, concat_axis=0, tiled=True)
        piece_out = expert_apply(arrived, w_gate, w_up, w_down).reshape(-1, model_width)
        reduced = lax.psum_scatter(piece_out, "tp", scatter_dimension=1, tiled=True)
        returned = send_back(reduced.reshape(req_count, share_rows, LANES))
        summed = returned.astype(jnp.float32).reshape(repeats, EXPERTS, share_rows, LANES).sum(
            axis=0
        )
        mixture_share = mixture_share + jnp.dot(
            combining_blocks[:, :, slots].reshape(tokens, EXPERTS * chunk_slots),
            summed.reshape(EXPERTS * chunk_slots, share_width),
            precision=lax.Precision.HIGHEST,
        )
    layer_out = jnp.where(live_rows[:, None], hidden_share + mixture_share, 0.0)
    return layer_out.astype(jnp.bfloat16)


def solution(mesh):
    return jax.shard_map(
        per_device,
        mesh=mesh,
        in_specs=(
            P("req", "tp"),
            P("req", None, "tp"),
            P("req", None, None, "tp"),
            P(),
            P("req"),
            P("req"),
            P("req", None),
            P(),
            P(),
            P("req", None),
            P("req", None, "tp"),
            P("req", None, "tp"),
            P("req", "tp", None),
            P("tp", None),
        ),
        out_specs=P("req", "tp"),
        check_vma=False,
    )
```

```python
import math

import jax
import jax.numpy as jnp
from jax import lax
from jax.sharding import PartitionSpec as P

HEADS = 32
KVH = 8
HD = 128
EXPERTS = 8
NPFX = 4
CAP = 18
LANES = 128
CHUNK_SLOTS = (12, 6)


def broadcast(x, axis, root):
    mine = lax.axis_index(axis) == root
    return lax.psum(jnp.where(mine, x, jnp.zeros_like(x)), axis)


def fetch_prefixes(prefix_cache, prefix_owner, request_prefix, req_count):
    plen = prefix_cache.shape[1]
    width = prefix_cache.shape[3]
    piece = plen // req_count
    requests = request_prefix.shape[0]
    pieces = prefix_cache.reshape(req_count, piece, 2, width)
    tag_rows = 16
    tags = jnp.zeros((tag_rows, 2, width), jnp.bfloat16)
    tags = tags.at[0, 0, :requests].set(request_prefix.astype(jnp.bfloat16))
    tagged = jnp.concatenate(
        [pieces, jnp.broadcast_to(tags[None], (req_count, tag_rows, 2, width))], axis=1
    )
    scattered = lax.all_to_all(tagged, "req", 0, 0, tiled=True)
    owner_pieces = jnp.take(scattered[:, :piece], prefix_owner, axis=0)
    wanted = scattered[:, piece, 0, :requests].astype(jnp.int32)
    outgoing = jnp.take(owner_pieces, wanted.reshape(-1), axis=0).reshape(
        req_count, requests, piece, 2, width
    )
    arrived = lax.all_to_all(outgoing, "req", 0, 0, tiled=True)
    return jnp.transpose(arrived, (1, 0, 2, 3, 4)).reshape(requests, plen, 2, width)


def tp_reduce_scatter(values, tp_count):
    rows, width = values.shape
    share = width // tp_count
    chunks = jnp.transpose(
        values.astype(jnp.bfloat16).reshape(rows, tp_count, share), (1, 0, 2)
    )
    arrived = lax.all_to_all(chunks, "tp", 0, 0, tiled=True)
    return arrived.astype(jnp.float32).sum(axis=0)


def tp_all_gather(share_values, tp_count):
    rows, share = share_values.shape
    copies = jnp.broadcast_to(share_values[None], (tp_count, rows, share))
    arrived = lax.all_to_all(copies, "tp", 0, 0, tiled=True)
    return jnp.transpose(arrived, (1, 0, 2)).reshape(rows, tp_count * share)


def attend_local(queries, suffix_kv, chosen, suffix_len, requests, slot_len):
    kv_local = suffix_kv.shape[2] // HD
    group_size = HEADS // KVH
    plen_local = chosen.shape[1]
    query_block = queries.reshape(requests, slot_len, kv_local, group_size, HD)
    cache_block = chosen.reshape(requests, plen_local, 2, kv_local, HD)
    suffix_block = suffix_kv.reshape(requests, slot_len, 2, kv_local, HD)
    score_scale = 1.0 / math.sqrt(HD)
    prefix_score = (
        jnp.einsum(
            "rikgd,rjkd->rkgij",
            query_block,
            cache_block[:, :, 0],
            preferred_element_type=jnp.float32,
        )
        * score_scale
    )
    suffix_score = (
        jnp.einsum(
            "rikgd,rjkd->rkgij",
            query_block,
            suffix_block[:, :, 0],
            preferred_element_type=jnp.float32,
        )
        * score_scale
    )
    positions = jnp.arange(slot_len, dtype=jnp.int32)
    allowed = (positions[None, None, :] <= positions[None, :, None]) & (
        positions[None, None, :] < suffix_len[:, None, None]
    )
    suffix_score = jnp.where(allowed[:, None, None], suffix_score, -1e30)
    score_peak = jnp.maximum(prefix_score.max(-1), suffix_score.max(-1))[..., None]
    prefix_exp = jnp.exp(prefix_score - score_peak)
    suffix_exp = jnp.exp(suffix_score - score_peak)
    normaliser = prefix_exp.sum(-1, keepdims=True) + suffix_exp.sum(-1, keepdims=True)
    prefix_prob = (prefix_exp / normaliser).astype(jnp.bfloat16)
    suffix_prob = (suffix_exp / normaliser).astype(jnp.bfloat16)
    mixed_values = jnp.einsum(
        "rkgij,rjkd->rikgd", prefix_prob, cache_block[:, :, 1], preferred_element_type=jnp.float32
    )
    mixed_values = mixed_values + jnp.einsum(
        "rkgij,rjkd->rikgd", suffix_prob, suffix_block[:, :, 1], preferred_element_type=jnp.float32
    )
    return mixed_values.reshape(requests * slot_len, kv_local * group_size * HD).astype(
        jnp.bfloat16
    )


def routing_tables(routes, live_rows, route_weight):
    expert_ids = jnp.arange(EXPERTS, dtype=jnp.int32)
    member = (routes[:, :, None] == expert_ids) & live_rows[:, None, None]
    member_int = member.astype(jnp.int32)
    flat_member = member_int.reshape(-1, EXPERTS)
    earlier = jnp.cumsum(flat_member, axis=0) - flat_member
    slot_index = jnp.sum(earlier * flat_member, axis=1).reshape(routes.shape)
    slot_hit = (slot_index[:, :, None] == jnp.arange(CAP, dtype=jnp.int32)).astype(jnp.float32)
    member_float = member.astype(jnp.float32)
    placing = (
        jnp.einsum("tke,tkc->ect", member_float, slot_hit)
        .reshape(EXPERTS * CAP, routes.shape[0])
        .astype(jnp.bfloat16)
    )
    combining = jnp.einsum(
        "tke,tkc,tk->tec", member_float, slot_hit, route_weight, precision=lax.Precision.HIGHEST
    )
    return (placing, combining.reshape(routes.shape[0], EXPERTS * CAP))


def expert_apply(arrived, w_gate, w_up, w_down):
    model_width = w_gate.shape[1]
    blocks = model_width // LANES
    packed = arrived.reshape(-1, blocks, LANES)
    gate_value = jnp.einsum(
        "rkl,klh->rh", packed, w_gate[0].reshape(blocks, LANES, -1),
        preferred_element_type=jnp.float32,
    )
    up_value = jnp.einsum(
        "rkl,klh->rh", packed, w_up[0].reshape(blocks, LANES, -1),
        preferred_element_type=jnp.float32,
    )
    hidden_units = (jax.nn.silu(gate_value) * up_value).astype(jnp.bfloat16)
    piece_out = jnp.dot(hidden_units, w_down[0], preferred_element_type=jnp.float32).astype(
        jnp.bfloat16
    )
    return piece_out.reshape(arrived.shape)


def send_back(parts):
    return lax.all_to_all(parts, "req", split_axis=0, concat_axis=0, tiled=True)


def per_device(
    queries,
    suffix_kv,
    prefix_cache,
    prefix_owner,
    request_prefix,
    suffix_len,
    residual,
    norm_gain,
    router,
    routes,
    w_gate,
    w_up,
    w_down,
    w_out,
):
    tp_count = lax.axis_size("tp")
    tp_index = lax.axis_index("tp")
    req_count = lax.axis_size("req")
    model_width = residual.shape[1]
    share_width = model_width // tp_count
    share_start = tp_index * share_width
    requests = request_prefix.shape[0]
    slot_len = queries.shape[0] // requests
    chosen = fetch_prefixes(prefix_cache, prefix_owner, request_prefix, req_count)
    attended = attend_local(queries, suffix_kv, chosen, suffix_len, requests, slot_len)
    partial_value = jnp.dot(attended, w_out, preferred_element_type=jnp.float32)
    attn_share = tp_reduce_scatter(partial_value, tp_count)
    attn_full = tp_all_gather(attn_share.astype(jnp.bfloat16), tp_count)
    hidden_state = residual.astype(jnp.float32) + attn_full.astype(jnp.float32)
    residual_share = lax.dynamic_slice_in_dim(residual, share_start, share_width, 1)
    hidden_share = residual_share.astype(jnp.float32) + attn_share
    inverse = lax.rsqrt(jnp.mean(hidden_state * hidden_state, axis=1, keepdims=True) + 1e-05)
    scaled = hidden_state * norm_gain * inverse
    logits = jnp.dot(scaled, router, precision=lax.Precision.HIGHEST)
    normed_full = scaled.astype(jnp.bfloat16)
    route_hit = (routes[:, :, None] == jnp.arange(EXPERTS, dtype=jnp.int32)).astype(jnp.float32)
    picked_logit = jnp.sum(route_hit * logits[:, None, :], axis=2)
    first_weight = jax.nn.sigmoid(picked_logit[:, 0] - picked_logit[:, 1])
    route_weight = jnp.stack([first_weight, 1.0 - first_weight], axis=1)
    live_rows = jnp.arange(routes.shape[0], dtype=jnp.int32) % slot_len < jnp.repeat(
        suffix_len, slot_len
    )
    placing, combining = routing_tables(routes, live_rows, route_weight)
    repeats = req_count // EXPERTS
    tokens = routes.shape[0]
    placing_blocks = placing.reshape(EXPERTS, CAP, tokens)
    combining_blocks = combining.reshape(tokens, EXPERTS, CAP)
    mixture_share = jnp.zeros((tokens, share_width), jnp.float32)
    first_slot = 0
    for chunk_slots in CHUNK_SLOTS:
        packed_rows = chunk_slots * model_width // LANES
        share_rows = chunk_slots * share_width // LANES
        slots = slice(first_slot, first_slot + chunk_slots)
        first_slot += chunk_slots
        chunk_placing = placing_blocks[:, slots].reshape(EXPERTS * chunk_slots, tokens)
        send_rows = jnp.dot(chunk_placing, normed_full, preferred_element_type=jnp.float32).astype(
            jnp.bfloat16
        )
        outgoing = jnp.tile(send_rows.reshape(EXPERTS, packed_rows, LANES), (repeats, 1, 1))
        arrived = lax.all_to_all(outgoing, "req", split_axis=0, concat_axis=0, tiled=True)
        piece_out = expert_apply(arrived, w_gate, w_up, w_down).reshape(-1, model_width)
        reduced = lax.psum_scatter(piece_out, "tp", scatter_dimension=1, tiled=True)
        returned = send_back(reduced.reshape(req_count, share_rows, LANES))
        summed = returned.astype(jnp.float32).reshape(repeats, EXPERTS, share_rows, LANES).sum(
            axis=0
        )
        mixture_share = mixture_share + jnp.dot(
            combining_blocks[:, :, slots].reshape(tokens, EXPERTS * chunk_slots),
            summed.reshape(EXPERTS * chunk_slots, share_width),
            precision=lax.Precision.HIGHEST,
        )
    layer_out = jnp.where(live_rows[:, None], hidden_share + mixture_share, 0.0)
    return layer_out.astype(jnp.bfloat16)


def solution(mesh):
    return jax.shard_map(
        per_device,
        mesh=mesh,
        in_specs=(
            P("req", "tp"),
            P("req", None, "tp"),
            P("req", None, None, "tp"),
            P(),
            P("req"),
            P("req"),
            P("req", None),
            P(),
            P(),
            P("req", None),
            P("req", None, "tp"),
            P("req", None, "tp"),
            P("req", "tp", None),
            P("tp", None),
        ),
        out_specs=P("req", "tp"),
        check_vma=False,
    )
```

```python
import math

import jax
import jax.numpy as jnp
from jax import lax
from jax.sharding import PartitionSpec as P

HEADS = 32
KVH = 8
HD = 128
EXPERTS = 8
NPFX = 4
CAP = 18
LANES = 128
CHUNK_SLOTS = (12, 6)


def broadcast(x, axis, root):
    mine = lax.axis_index(axis) == root
    return lax.psum(jnp.where(mine, x, jnp.zeros_like(x)), axis)


def fetch_prefixes(prefix_cache, prefix_owner, request_prefix, req_count):
    plen = prefix_cache.shape[1]
    width = prefix_cache.shape[3]
    piece = plen // req_count
    requests = request_prefix.shape[0]
    pieces = prefix_cache.reshape(req_count, piece, 2, width)
    tag_rows = 16
    tags = jnp.zeros((tag_rows, 2, width), jnp.bfloat16)
    tags = tags.at[0, 0, :requests].set(request_prefix.astype(jnp.bfloat16))
    tagged = jnp.concatenate(
        [pieces, jnp.broadcast_to(tags[None], (req_count, tag_rows, 2, width))], axis=1
    )
    scattered = lax.all_to_all(tagged, "req", 0, 0, tiled=True)
    wanted = scattered[:, piece, 0, :requests].astype(jnp.int32)
    sources = jnp.take(prefix_owner, wanted.reshape(-1), axis=0)
    outgoing = jnp.take(scattered, sources, axis=0)[:, :piece].reshape(
        req_count, requests, piece, 2, width
    )
    arrived = lax.all_to_all(outgoing, "req", 0, 0, tiled=True)
    return jnp.transpose(arrived, (1, 0, 2, 3, 4)).reshape(requests, plen, 2, width)


def tp_reduce_scatter(values, tp_count):
    rows, width = values.shape
    share = width // tp_count
    chunks = jnp.transpose(
        values.astype(jnp.bfloat16).reshape(rows, tp_count, share), (1, 0, 2)
    )
    arrived = lax.all_to_all(chunks, "tp", 0, 0, tiled=True)
    return arrived.astype(jnp.float32).sum(axis=0)


def tp_all_gather(share_values, tp_count):
    rows, share = share_values.shape
    copies = jnp.broadcast_to(share_values[None], (tp_count, rows, share))
    arrived = lax.all_to_all(copies, "tp", 0, 0, tiled=True)
    return jnp.transpose(arrived, (1, 0, 2)).reshape(rows, tp_count * share)


def attend_local(queries, suffix_kv, chosen, suffix_len, requests, slot_len):
    kv_local = suffix_kv.shape[2] // HD
    group_size = HEADS // KVH
    plen_local = chosen.shape[1]
    query_block = queries.reshape(requests, slot_len, kv_local, group_size, HD)
    cache_block = chosen.reshape(requests, plen_local, 2, kv_local, HD)
    suffix_block = suffix_kv.reshape(requests, slot_len, 2, kv_local, HD)
    score_scale = 1.0 / math.sqrt(HD)
    prefix_score = (
        jnp.einsum(
            "rikgd,rjkd->rkgij",
            query_block,
            cache_block[:, :, 0],
            preferred_element_type=jnp.float32,
        )
        * score_scale
    )
    suffix_score = (
        jnp.einsum(
            "rikgd,rjkd->rkgij",
            query_block,
            suffix_block[:, :, 0],
            preferred_element_type=jnp.float32,
        )
        * score_scale
    )
    positions = jnp.arange(slot_len, dtype=jnp.int32)
    allowed = (positions[None, None, :] <= positions[None, :, None]) & (
        positions[None, None, :] < suffix_len[:, None, None]
    )
    suffix_score = jnp.where(allowed[:, None, None], suffix_score, -1e30)
    score_peak = jnp.maximum(prefix_score.max(-1), suffix_score.max(-1))[..., None]
    prefix_exp = jnp.exp(prefix_score - score_peak)
    suffix_exp = jnp.exp(suffix_score - score_peak)
    normaliser = prefix_exp.sum(-1, keepdims=True) + suffix_exp.sum(-1, keepdims=True)
    prefix_prob = (prefix_exp / normaliser).astype(jnp.bfloat16)
    suffix_prob = (suffix_exp / normaliser).astype(jnp.bfloat16)
    mixed_values = jnp.einsum(
        "rkgij,rjkd->rikgd", prefix_prob, cache_block[:, :, 1], preferred_element_type=jnp.float32
    )
    mixed_values = mixed_values + jnp.einsum(
        "rkgij,rjkd->rikgd", suffix_prob, suffix_block[:, :, 1], preferred_element_type=jnp.float32
    )
    return mixed_values.reshape(requests * slot_len, kv_local * group_size * HD).astype(
        jnp.bfloat16
    )


def routing_tables(routes, live_rows, route_weight):
    expert_ids = jnp.arange(EXPERTS, dtype=jnp.int32)
    member = (routes[:, :, None] == expert_ids) & live_rows[:, None, None]
    member_int = member.astype(jnp.int32)
    flat_member = member_int.reshape(-1, EXPERTS)
    earlier = jnp.cumsum(flat_member, axis=0) - flat_member
    slot_index = jnp.sum(earlier * flat_member, axis=1).reshape(routes.shape)
    slot_hit = (slot_index[:, :, None] == jnp.arange(CAP, dtype=jnp.int32)).astype(jnp.float32)
    member_float = member.astype(jnp.float32)
    placing = (
        jnp.einsum("tke,tkc->ect", member_float, slot_hit)
        .reshape(EXPERTS * CAP, routes.shape[0])
        .astype(jnp.bfloat16)
    )
    combining = jnp.einsum(
        "tke,tkc,tk->tec", member_float, slot_hit, route_weight, precision=lax.Precision.HIGHEST
    )
    return (placing, combining.reshape(routes.shape[0], EXPERTS * CAP))


def expert_apply(arrived, w_gate, w_up, w_down):
    model_width = w_gate.shape[1]
    blocks = model_width // LANES
    packed = arrived.reshape(-1, blocks, LANES)
    gate_value = jnp.einsum(
        "rkl,klh->rh", packed, w_gate[0].reshape(blocks, LANES, -1),
        preferred_element_type=jnp.float32,
    )
    up_value = jnp.einsum(
        "rkl,klh->rh", packed, w_up[0].reshape(blocks, LANES, -1),
        preferred_element_type=jnp.float32,
    )
    hidden_units = (jax.nn.silu(gate_value) * up_value).astype(jnp.bfloat16)
    piece_out = jnp.dot(hidden_units, w_down[0], preferred_element_type=jnp.float32).astype(
        jnp.bfloat16
    )
    return piece_out.reshape(arrived.shape)


def send_back(parts):
    return lax.all_to_all(parts, "req", split_axis=0, concat_axis=0, tiled=True)


def per_device(
    queries,
    suffix_kv,
    prefix_cache,
    prefix_owner,
    request_prefix,
    suffix_len,
    residual,
    norm_gain,
    router,
    routes,
    w_gate,
    w_up,
    w_down,
    w_out,
):
    tp_count = lax.axis_size("tp")
    tp_index = lax.axis_index("tp")
    req_count = lax.axis_size("req")
    model_width = residual.shape[1]
    share_width = model_width // tp_count
    share_start = tp_index * share_width
    requests = request_prefix.shape[0]
    slot_len = queries.shape[0] // requests
    chosen = fetch_prefixes(prefix_cache, prefix_owner, request_prefix, req_count)
    attended = attend_local(queries, suffix_kv, chosen, suffix_len, requests, slot_len)
    partial_value = jnp.dot(attended, w_out, preferred_element_type=jnp.float32)
    attn_share = tp_reduce_scatter(partial_value, tp_count)
    attn_full = tp_all_gather(attn_share.astype(jnp.bfloat16), tp_count)
    hidden_state = residual.astype(jnp.float32) + attn_full.astype(jnp.float32)
    residual_share = lax.dynamic_slice_in_dim(residual, share_start, share_width, 1)
    hidden_share = residual_share.astype(jnp.float32) + attn_share
    inverse = lax.rsqrt(jnp.mean(hidden_state * hidden_state, axis=1, keepdims=True) + 1e-05)
    scaled = hidden_state * norm_gain * inverse
    logits = jnp.dot(scaled, router, precision=lax.Precision.HIGHEST)
    normed_full = scaled.astype(jnp.bfloat16)
    route_hit = (routes[:, :, None] == jnp.arange(EXPERTS, dtype=jnp.int32)).astype(jnp.float32)
    picked_logit = jnp.sum(route_hit * logits[:, None, :], axis=2)
    first_weight = jax.nn.sigmoid(picked_logit[:, 0] - picked_logit[:, 1])
    route_weight = jnp.stack([first_weight, 1.0 - first_weight], axis=1)
    live_rows = jnp.arange(routes.shape[0], dtype=jnp.int32) % slot_len < jnp.repeat(
        suffix_len, slot_len
    )
    placing, combining = routing_tables(routes, live_rows, route_weight)
    repeats = req_count // EXPERTS
    tokens = routes.shape[0]
    placing_blocks = placing.reshape(EXPERTS, CAP, tokens)
    normed_packed = normed_full.reshape(tokens, model_width // LANES, LANES)
    combining_blocks = combining.reshape(tokens, EXPERTS, CAP)
    mixture_share = jnp.zeros((tokens, share_width), jnp.float32)
    first_slot = 0
    for chunk_slots in CHUNK_SLOTS:
        packed_rows = chunk_slots * model_width // LANES
        share_rows = chunk_slots * share_width // LANES
        slots = slice(first_slot, first_slot + chunk_slots)
        first_slot += chunk_slots
        chunk_placing = jnp.tile(
            placing_blocks[:, slots].reshape(EXPERTS * chunk_slots, tokens), (repeats, 1)
        )
        send_rows = jnp.einsum(
            "ct,tkl->ckl", chunk_placing, normed_packed, preferred_element_type=jnp.float32
        ).astype(jnp.bfloat16)
        outgoing = send_rows.reshape(req_count, packed_rows, LANES)
        arrived = lax.all_to_all(outgoing, "req", split_axis=0, concat_axis=0, tiled=True)
        piece_out = expert_apply(arrived, w_gate, w_up, w_down).reshape(-1, model_width)
        reduced = lax.psum_scatter(piece_out, "tp", scatter_dimension=1, tiled=True)
        returned = send_back(reduced.reshape(req_count, share_rows, LANES))
        summed = returned.astype(jnp.float32).reshape(repeats, EXPERTS, share_rows, LANES).sum(
            axis=0
        )
        mixture_share = mixture_share + jnp.dot(
            combining_blocks[:, :, slots].reshape(tokens, EXPERTS * chunk_slots),
            summed.reshape(EXPERTS * chunk_slots, share_width),
            precision=lax.Precision.HIGHEST,
        )
    layer_out = jnp.where(live_rows[:, None], hidden_share + mixture_share, 0.0)
    return layer_out.astype(jnp.bfloat16)


def solution(mesh):
    return jax.shard_map(
        per_device,
        mesh=mesh,
        in_specs=(
            P("req", "tp"),
            P("req", None, "tp"),
            P("req", None, None, "tp"),
            P(),
            P("req"),
            P("req"),
            P("req", None),
            P(),
            P(),
            P("req", None),
            P("req", None, "tp"),
            P("req", None, "tp"),
            P("req", "tp", None),
            P("tp", None),
        ),
        out_specs=P("req", "tp"),
        check_vma=False,
    )
```

```python
import math

import jax
import jax.numpy as jnp
from jax import lax
from jax.sharding import PartitionSpec as P

HEADS = 32
KVH = 8
HD = 128
EXPERTS = 8
NPFX = 4
CAP = 18
LANES = 128
CHUNK_SLOTS = (6, 6, 6)


def broadcast(x, axis, root):
    mine = lax.axis_index(axis) == root
    return lax.psum(jnp.where(mine, x, jnp.zeros_like(x)), axis)


def fetch_prefixes(prefix_cache, prefix_owner, request_prefix, req_count):
    plen = prefix_cache.shape[1]
    width = prefix_cache.shape[3]
    piece = plen // req_count
    requests = request_prefix.shape[0]
    pieces = prefix_cache.reshape(req_count, piece, 2, width)
    tag_rows = 16
    tags = jnp.zeros((tag_rows, 2, width), jnp.bfloat16)
    tags = tags.at[0, 0, :requests].set(request_prefix.astype(jnp.bfloat16))
    tagged = jnp.concatenate(
        [pieces, jnp.broadcast_to(tags[None], (req_count, tag_rows, 2, width))], axis=1
    )
    scattered = lax.all_to_all(tagged, "req", 0, 0, tiled=True)
    wanted = scattered[:, piece, 0, :requests].astype(jnp.int32)
    sources = jnp.take(prefix_owner, wanted.reshape(-1), axis=0)
    outgoing = jnp.take(scattered, sources, axis=0)[:, :piece].reshape(
        req_count, requests, piece, 2, width
    )
    arrived = lax.all_to_all(outgoing, "req", 0, 0, tiled=True)
    return jnp.transpose(arrived, (1, 0, 2, 3, 4)).reshape(requests, plen, 2, width)


def tp_reduce_scatter(values, tp_count):
    rows, width = values.shape
    share = width // tp_count
    chunks = jnp.transpose(
        values.astype(jnp.bfloat16).reshape(rows, tp_count, share), (1, 0, 2)
    )
    arrived = lax.all_to_all(chunks, "tp", 0, 0, tiled=True)
    return arrived.astype(jnp.float32).sum(axis=0)


def tp_all_gather(share_values, tp_count):
    rows, share = share_values.shape
    copies = jnp.broadcast_to(share_values[None], (tp_count, rows, share))
    arrived = lax.all_to_all(copies, "tp", 0, 0, tiled=True)
    return jnp.transpose(arrived, (1, 0, 2)).reshape(rows, tp_count * share)


def attend_local(queries, suffix_kv, chosen, suffix_len, requests, slot_len):
    kv_local = suffix_kv.shape[2] // HD
    group_size = HEADS // KVH
    plen_local = chosen.shape[1]
    query_block = queries.reshape(requests, slot_len, kv_local, group_size, HD)
    cache_block = chosen.reshape(requests, plen_local, 2, kv_local, HD)
    suffix_block = suffix_kv.reshape(requests, slot_len, 2, kv_local, HD)
    score_scale = 1.0 / math.sqrt(HD)
    prefix_score = (
        jnp.einsum(
            "rikgd,rjkd->rkgij",
            query_block,
            cache_block[:, :, 0],
            preferred_element_type=jnp.float32,
        )
        * score_scale
    )
    suffix_score = (
        jnp.einsum(
            "rikgd,rjkd->rkgij",
            query_block,
            suffix_block[:, :, 0],
            preferred_element_type=jnp.float32,
        )
        * score_scale
    )
    positions = jnp.arange(slot_len, dtype=jnp.int32)
    allowed = (positions[None, None, :] <= positions[None, :, None]) & (
        positions[None, None, :] < suffix_len[:, None, None]
    )
    suffix_score = jnp.where(allowed[:, None, None], suffix_score, -1e30)
    score_peak = jnp.maximum(prefix_score.max(-1), suffix_score.max(-1))[..., None]
    prefix_exp = jnp.exp(prefix_score - score_peak)
    suffix_exp = jnp.exp(suffix_score - score_peak)
    normaliser = prefix_exp.sum(-1, keepdims=True) + suffix_exp.sum(-1, keepdims=True)
    prefix_prob = (prefix_exp / normaliser).astype(jnp.bfloat16)
    suffix_prob = (suffix_exp / normaliser).astype(jnp.bfloat16)
    mixed_values = jnp.einsum(
        "rkgij,rjkd->rikgd", prefix_prob, cache_block[:, :, 1], preferred_element_type=jnp.float32
    )
    mixed_values = mixed_values + jnp.einsum(
        "rkgij,rjkd->rikgd", suffix_prob, suffix_block[:, :, 1], preferred_element_type=jnp.float32
    )
    return mixed_values.reshape(requests * slot_len, kv_local * group_size * HD).astype(
        jnp.bfloat16
    )


def routing_tables(routes, live_rows, route_weight):
    expert_ids = jnp.arange(EXPERTS, dtype=jnp.int32)
    member = (routes[:, :, None] == expert_ids) & live_rows[:, None, None]
    member_int = member.astype(jnp.int32)
    flat_member = member_int.reshape(-1, EXPERTS)
    earlier = jnp.cumsum(flat_member, axis=0) - flat_member
    slot_index = jnp.sum(earlier * flat_member, axis=1).reshape(routes.shape)
    slot_hit = (slot_index[:, :, None] == jnp.arange(CAP, dtype=jnp.int32)).astype(jnp.float32)
    member_float = member.astype(jnp.float32)
    placing = (
        jnp.einsum("tke,tkc->ect", member_float, slot_hit)
        .reshape(EXPERTS * CAP, routes.shape[0])
        .astype(jnp.bfloat16)
    )
    combining = jnp.einsum(
        "tke,tkc,tk->tec", member_float, slot_hit, route_weight, precision=lax.Precision.HIGHEST
    )
    return (placing, combining.reshape(routes.shape[0], EXPERTS * CAP))


def expert_apply(arrived, w_gate, w_up, w_down):
    model_width = w_gate.shape[1]
    blocks = model_width // LANES
    packed = arrived.reshape(-1, blocks, LANES)
    gate_value = jnp.einsum(
        "rkl,klh->rh", packed, w_gate[0].reshape(blocks, LANES, -1),
        preferred_element_type=jnp.float32,
    )
    up_value = jnp.einsum(
        "rkl,klh->rh", packed, w_up[0].reshape(blocks, LANES, -1),
        preferred_element_type=jnp.float32,
    )
    hidden_units = (jax.nn.silu(gate_value) * up_value).astype(jnp.bfloat16)
    piece_out = jnp.dot(hidden_units, w_down[0], preferred_element_type=jnp.float32).astype(
        jnp.bfloat16
    )
    return piece_out.reshape(arrived.shape)


def send_back(parts):
    return lax.all_to_all(parts, "req", split_axis=0, concat_axis=0, tiled=True)


def per_device(
    queries,
    suffix_kv,
    prefix_cache,
    prefix_owner,
    request_prefix,
    suffix_len,
    residual,
    norm_gain,
    router,
    routes,
    w_gate,
    w_up,
    w_down,
    w_out,
):
    tp_count = lax.axis_size("tp")
    tp_index = lax.axis_index("tp")
    req_count = lax.axis_size("req")
    model_width = residual.shape[1]
    share_width = model_width // tp_count
    share_start = tp_index * share_width
    requests = request_prefix.shape[0]
    slot_len = queries.shape[0] // requests
    chosen = fetch_prefixes(prefix_cache, prefix_owner, request_prefix, req_count)
    attended = attend_local(queries, suffix_kv, chosen, suffix_len, requests, slot_len)
    partial_value = jnp.dot(attended, w_out, preferred_element_type=jnp.float32)
    attn_share = tp_reduce_scatter(partial_value, tp_count)
    attn_full = tp_all_gather(attn_share.astype(jnp.bfloat16), tp_count)
    hidden_state = residual.astype(jnp.float32) + attn_full.astype(jnp.float32)
    residual_share = lax.dynamic_slice_in_dim(residual, share_start, share_width, 1)
    hidden_share = residual_share.astype(jnp.float32) + attn_share
    inverse = lax.rsqrt(jnp.mean(hidden_state * hidden_state, axis=1, keepdims=True) + 1e-05)
    scaled = hidden_state * norm_gain * inverse
    logits = jnp.dot(scaled, router, precision=lax.Precision.HIGHEST)
    normed_full = scaled.astype(jnp.bfloat16)
    route_hit = (routes[:, :, None] == jnp.arange(EXPERTS, dtype=jnp.int32)).astype(jnp.float32)
    picked_logit = jnp.sum(route_hit * logits[:, None, :], axis=2)
    first_weight = jax.nn.sigmoid(picked_logit[:, 0] - picked_logit[:, 1])
    route_weight = jnp.stack([first_weight, 1.0 - first_weight], axis=1)
    live_rows = jnp.arange(routes.shape[0], dtype=jnp.int32) % slot_len < jnp.repeat(
        suffix_len, slot_len
    )
    placing, combining = routing_tables(routes, live_rows, route_weight)
    repeats = req_count // EXPERTS
    tokens = routes.shape[0]
    placing_blocks = placing.reshape(EXPERTS, CAP, tokens)
    normed_packed = normed_full.reshape(tokens, model_width // LANES, LANES)
    combining_blocks = combining.reshape(tokens, EXPERTS, CAP)
    mixture_share = jnp.zeros((tokens, share_width), jnp.float32)
    first_slot = 0
    for chunk_slots in CHUNK_SLOTS:
        packed_rows = chunk_slots * model_width // LANES
        share_rows = chunk_slots * share_width // LANES
        slots = slice(first_slot, first_slot + chunk_slots)
        first_slot += chunk_slots
        chunk_placing = jnp.tile(
            placing_blocks[:, slots].reshape(EXPERTS * chunk_slots, tokens), (repeats, 1)
        )
        send_rows = jnp.einsum(
            "ct,tkl->ckl", chunk_placing, normed_packed, preferred_element_type=jnp.float32
        ).astype(jnp.bfloat16)
        outgoing = send_rows.reshape(req_count, packed_rows, LANES)
        arrived = lax.all_to_all(outgoing, "req", split_axis=0, concat_axis=0, tiled=True)
        piece_out = expert_apply(arrived, w_gate, w_up, w_down).reshape(-1, model_width)
        reduced = lax.psum_scatter(piece_out, "tp", scatter_dimension=1, tiled=True)
        returned = send_back(reduced.reshape(req_count, share_rows, LANES))
        summed = returned.astype(jnp.float32).reshape(repeats, EXPERTS, share_rows, LANES).sum(
            axis=0
        )
        mixture_share = mixture_share + jnp.dot(
            combining_blocks[:, :, slots].reshape(tokens, EXPERTS * chunk_slots),
            summed.reshape(EXPERTS * chunk_slots, share_width),
            precision=lax.Precision.HIGHEST,
        )
    layer_out = jnp.where(live_rows[:, None], hidden_share + mixture_share, 0.0)
    return layer_out.astype(jnp.bfloat16)


def solution(mesh):
    return jax.shard_map(
        per_device,
        mesh=mesh,
        in_specs=(
            P("req", "tp"),
            P("req", None, "tp"),
            P("req", None, None, "tp"),
            P(),
            P("req"),
            P("req"),
            P("req", None),
            P(),
            P(),
            P("req", None),
            P("req", None, "tp"),
            P("req", None, "tp"),
            P("req", "tp", None),
            P("tp", None),
        ),
        out_specs=P("req", "tp"),
        check_vma=False,
    )
```

```python
import math

import jax
import jax.numpy as jnp
from jax import lax
from jax.sharding import PartitionSpec as P

HEADS = 32
KVH = 8
HD = 128
EXPERTS = 8
NPFX = 4
CAP = 18
LANES = 128
CHUNK_SLOTS = (12, 6)


def broadcast(x, axis, root):
    mine = lax.axis_index(axis) == root
    return lax.psum(jnp.where(mine, x, jnp.zeros_like(x)), axis)


def fetch_prefixes(prefix_cache, prefix_owner, request_prefix, req_count):
    plen = prefix_cache.shape[1]
    width = prefix_cache.shape[3]
    piece = plen // req_count
    requests = request_prefix.shape[0]
    pieces = prefix_cache.reshape(req_count, piece, 2, width)
    tag_rows = 16
    tags = jnp.zeros((tag_rows, 2, width), jnp.bfloat16)
    tags = tags.at[0, 0, :requests].set(request_prefix.astype(jnp.bfloat16))
    tagged = jnp.concatenate(
        [pieces, jnp.broadcast_to(tags[None], (req_count, tag_rows, 2, width))], axis=1
    )
    scattered = lax.all_to_all(tagged, "req", 0, 0, tiled=True)
    wanted = scattered[:, piece, 0, :requests].astype(jnp.int32)
    sources = jnp.take(prefix_owner, wanted.reshape(-1), axis=0)
    outgoing = jnp.take(scattered, sources, axis=0)[:, :piece].reshape(
        req_count, requests, piece, 2, width
    )
    arrived = lax.all_to_all(outgoing, "req", 0, 0, tiled=True)
    return jnp.transpose(arrived, (1, 0, 2, 3, 4)).reshape(requests, plen, 2, width)


def tp_reduce_scatter(values, tp_count):
    rows, width = values.shape
    share = width // tp_count
    chunks = jnp.transpose(
        values.astype(jnp.bfloat16).reshape(rows, tp_count, share), (1, 0, 2)
    )
    arrived = lax.all_to_all(chunks, "tp", 0, 0, tiled=True)
    return arrived.astype(jnp.float32).sum(axis=0)


def tp_all_gather(share_values, tp_count):
    rows, share = share_values.shape
    copies = jnp.broadcast_to(share_values[None], (tp_count, rows, share))
    arrived = lax.all_to_all(copies, "tp", 0, 0, tiled=True)
    return jnp.transpose(arrived, (1, 0, 2)).reshape(rows, tp_count * share)


def attend_local(queries, suffix_kv, chosen, suffix_len, requests, slot_len):
    kv_local = suffix_kv.shape[2] // HD
    group_size = HEADS // KVH
    plen_local = chosen.shape[1]
    query_block = queries.reshape(requests, slot_len, kv_local, group_size, HD)
    cache_block = chosen.reshape(requests, plen_local, 2, kv_local, HD)
    suffix_block = suffix_kv.reshape(requests, slot_len, 2, kv_local, HD)
    score_scale = 1.0 / math.sqrt(HD)
    prefix_score = (
        jnp.einsum(
            "rikgd,rjkd->rkgij",
            query_block,
            cache_block[:, :, 0],
            preferred_element_type=jnp.float32,
        )
        * score_scale
    )
    suffix_score = (
        jnp.einsum(
            "rikgd,rjkd->rkgij",
            query_block,
            suffix_block[:, :, 0],
            preferred_element_type=jnp.float32,
        )
        * score_scale
    )
    positions = jnp.arange(slot_len, dtype=jnp.int32)
    allowed = (positions[None, None, :] <= positions[None, :, None]) & (
        positions[None, None, :] < suffix_len[:, None, None]
    )
    suffix_score = jnp.where(allowed[:, None, None], suffix_score, -1e30)
    score_peak = jnp.maximum(prefix_score.max(-1), suffix_score.max(-1))[..., None]
    prefix_exp = jnp.exp(prefix_score - score_peak)
    suffix_exp = jnp.exp(suffix_score - score_peak)
    normaliser = prefix_exp.sum(-1, keepdims=True) + suffix_exp.sum(-1, keepdims=True)
    prefix_prob = (prefix_exp / normaliser).astype(jnp.bfloat16)
    suffix_prob = (suffix_exp / normaliser).astype(jnp.bfloat16)
    mixed_values = jnp.einsum(
        "rkgij,rjkd->rikgd", prefix_prob, cache_block[:, :, 1], preferred_element_type=jnp.float32
    )
    mixed_values = mixed_values + jnp.einsum(
        "rkgij,rjkd->rikgd", suffix_prob, suffix_block[:, :, 1], preferred_element_type=jnp.float32
    )
    return mixed_values.reshape(requests * slot_len, kv_local * group_size * HD).astype(
        jnp.bfloat16
    )


def routing_tables(routes, live_rows, route_weight):
    expert_ids = jnp.arange(EXPERTS, dtype=jnp.int32)
    member = (routes[:, :, None] == expert_ids) & live_rows[:, None, None]
    member_int = member.astype(jnp.int32)
    flat_member = member_int.reshape(-1, EXPERTS)
    earlier = jnp.cumsum(flat_member, axis=0) - flat_member
    slot_index = jnp.sum(earlier * flat_member, axis=1).reshape(routes.shape)
    slot_hit = (slot_index[:, :, None] == jnp.arange(CAP, dtype=jnp.int32)).astype(jnp.float32)
    member_float = member.astype(jnp.float32)
    placing = (
        jnp.einsum("tke,tkc->ect", member_float, slot_hit)
        .reshape(EXPERTS * CAP, routes.shape[0])
        .astype(jnp.bfloat16)
    )
    combining = jnp.einsum(
        "tke,tkc,tk->tec", member_float, slot_hit, route_weight, precision=lax.Precision.HIGHEST
    )
    return (placing, combining.reshape(routes.shape[0], EXPERTS * CAP))


def expert_apply(arrived, w_gate, w_up, w_down):
    model_width = w_gate.shape[1]
    blocks = model_width // LANES
    packed = arrived.reshape(-1, blocks, LANES)
    gate_value = jnp.einsum(
        "rkl,klh->rh", packed, w_gate[0].reshape(blocks, LANES, -1),
        preferred_element_type=jnp.float32,
    )
    up_value = jnp.einsum(
        "rkl,klh->rh", packed, w_up[0].reshape(blocks, LANES, -1),
        preferred_element_type=jnp.float32,
    )
    hidden_units = (jax.nn.silu(gate_value) * up_value).astype(jnp.bfloat16)
    piece_out = jnp.dot(hidden_units, w_down[0], preferred_element_type=jnp.float32).astype(
        jnp.bfloat16
    )
    return piece_out.reshape(arrived.shape)


def send_back(parts):
    return lax.all_to_all(parts, "req", split_axis=0, concat_axis=0, tiled=True)


def per_device(
    queries,
    suffix_kv,
    prefix_cache,
    prefix_owner,
    request_prefix,
    suffix_len,
    residual,
    norm_gain,
    router,
    routes,
    w_gate,
    w_up,
    w_down,
    w_out,
):
    tp_count = lax.axis_size("tp")
    tp_index = lax.axis_index("tp")
    req_count = lax.axis_size("req")
    model_width = residual.shape[1]
    share_width = model_width // tp_count
    share_start = tp_index * share_width
    requests = request_prefix.shape[0]
    slot_len = queries.shape[0] // requests
    chosen = fetch_prefixes(prefix_cache, prefix_owner, request_prefix, req_count)
    attended = attend_local(queries, suffix_kv, chosen, suffix_len, requests, slot_len)
    partial_value = jnp.dot(attended, w_out, preferred_element_type=jnp.float32)
    attn_share = tp_reduce_scatter(partial_value, tp_count)
    attn_full = tp_all_gather(attn_share.astype(jnp.bfloat16), tp_count)
    hidden_state = residual.astype(jnp.float32) + attn_full.astype(jnp.float32)
    residual_share = lax.dynamic_slice_in_dim(residual, share_start, share_width, 1)
    hidden_share = residual_share.astype(jnp.float32) + attn_share
    inverse = lax.rsqrt(jnp.mean(hidden_state * hidden_state, axis=1, keepdims=True) + 1e-05)
    scaled = hidden_state * norm_gain * inverse
    logits = jnp.dot(scaled, router, precision=lax.Precision.HIGHEST)
    normed_full = scaled.astype(jnp.bfloat16)
    route_hit = (routes[:, :, None] == jnp.arange(EXPERTS, dtype=jnp.int32)).astype(jnp.float32)
    picked_logit = jnp.sum(route_hit * logits[:, None, :], axis=2)
    first_weight = jax.nn.sigmoid(picked_logit[:, 0] - picked_logit[:, 1])
    route_weight = jnp.stack([first_weight, 1.0 - first_weight], axis=1)
    live_rows = jnp.arange(routes.shape[0], dtype=jnp.int32) % slot_len < jnp.repeat(
        suffix_len, slot_len
    )
    placing, combining = routing_tables(routes, live_rows, route_weight)
    repeats = req_count // EXPERTS
    tokens = routes.shape[0]
    placing_blocks = placing.reshape(EXPERTS, CAP, tokens)
    normed_packed = normed_full.reshape(tokens, model_width // LANES, LANES)
    combining_blocks = combining.reshape(tokens, EXPERTS, CAP)
    mixture_share = jnp.zeros((tokens, share_width), jnp.float32)
    first_slot = 0
    for chunk_slots in CHUNK_SLOTS:
        packed_rows = chunk_slots * model_width // LANES
        share_rows = chunk_slots * share_width // LANES
        slots = slice(first_slot, first_slot + chunk_slots)
        first_slot += chunk_slots
        chunk_placing = jnp.tile(
            placing_blocks[:, slots].reshape(EXPERTS * chunk_slots, tokens), (repeats, 1)
        )
        send_rows = jnp.einsum(
            "ct,tkl->ckl", chunk_placing, normed_packed, preferred_element_type=jnp.float32
        ).astype(jnp.bfloat16)
        outgoing = send_rows.reshape(req_count, packed_rows, LANES)
        arrived = lax.all_to_all(outgoing, "req", split_axis=0, concat_axis=0, tiled=True)
        piece_out = expert_apply(arrived, w_gate, w_up, w_down).reshape(-1, model_width)
        reduced = lax.psum_scatter(piece_out, "tp", scatter_dimension=1, tiled=True)
        returned = send_back(reduced.reshape(req_count, share_rows, LANES))
        summed = returned.astype(jnp.float32).reshape(repeats, EXPERTS, share_rows, LANES).sum(
            axis=0
        )
        mixture_share = mixture_share + jnp.dot(
            combining_blocks[:, :, slots].reshape(tokens, EXPERTS * chunk_slots),
            summed.reshape(EXPERTS * chunk_slots, share_width),
            precision=lax.Precision.HIGH,
        )
    layer_out = jnp.where(live_rows[:, None], hidden_share + mixture_share, 0.0)
    return layer_out.astype(jnp.bfloat16)


def solution(mesh):
    return jax.shard_map(
        per_device,
        mesh=mesh,
        in_specs=(
            P("req", "tp"),
            P("req", None, "tp"),
            P("req", None, None, "tp"),
            P(),
            P("req"),
            P("req"),
            P("req", None),
            P(),
            P(),
            P("req", None),
            P("req", None, "tp"),
            P("req", None, "tp"),
            P("req", "tp", None),
            P("tp", None),
        ),
        out_specs=P("req", "tp"),
        check_vma=False,
    )
```

```python
import math

import jax
import jax.numpy as jnp
from jax import lax
from jax.sharding import PartitionSpec as P

HEADS = 32
KVH = 8
HD = 128
EXPERTS = 8
NPFX = 4
CAP = 18
LANES = 128
CHUNK_SLOTS = (11, 7)


def broadcast(x, axis, root):
    mine = lax.axis_index(axis) == root
    return lax.psum(jnp.where(mine, x, jnp.zeros_like(x)), axis)


def fetch_prefixes(prefix_cache, prefix_owner, request_prefix, req_count):
    plen = prefix_cache.shape[1]
    width = prefix_cache.shape[3]
    piece = plen // req_count
    requests = request_prefix.shape[0]
    pieces = prefix_cache.reshape(req_count, piece, 2, width)
    tag_rows = 16
    tags = jnp.zeros((tag_rows, 2, width), jnp.bfloat16)
    tags = tags.at[0, 0, :requests].set(request_prefix.astype(jnp.bfloat16))
    tagged = jnp.concatenate(
        [pieces, jnp.broadcast_to(tags[None], (req_count, tag_rows, 2, width))], axis=1
    )
    scattered = lax.all_to_all(tagged, "req", 0, 0, tiled=True)
    wanted = scattered[:, piece, 0, :requests].astype(jnp.int32)
    sources = jnp.take(prefix_owner, wanted.reshape(-1), axis=0)
    outgoing = jnp.take(scattered, sources, axis=0)[:, :piece].reshape(
        req_count, requests, piece, 2, width
    )
    arrived = lax.all_to_all(outgoing, "req", 0, 0, tiled=True)
    return jnp.transpose(arrived, (1, 0, 2, 3, 4)).reshape(requests, plen, 2, width)


def tp_reduce_scatter(values, tp_count):
    rows, width = values.shape
    share = width // tp_count
    chunks = jnp.transpose(
        values.astype(jnp.bfloat16).reshape(rows, tp_count, share), (1, 0, 2)
    )
    arrived = lax.all_to_all(chunks, "tp", 0, 0, tiled=True)
    return arrived.astype(jnp.float32).sum(axis=0)


def tp_all_gather(share_values, tp_count):
    rows, share = share_values.shape
    copies = jnp.broadcast_to(share_values[None], (tp_count, rows, share))
    arrived = lax.all_to_all(copies, "tp", 0, 0, tiled=True)
    return jnp.transpose(arrived, (1, 0, 2)).reshape(rows, tp_count * share)


def attend_local(queries, suffix_kv, chosen, suffix_len, requests, slot_len):
    kv_local = suffix_kv.shape[2] // HD
    group_size = HEADS // KVH
    plen_local = chosen.shape[1]
    query_block = queries.reshape(requests, slot_len, kv_local, group_size, HD)
    cache_block = chosen.reshape(requests, plen_local, 2, kv_local, HD)
    suffix_block = suffix_kv.reshape(requests, slot_len, 2, kv_local, HD)
    score_scale = 1.0 / math.sqrt(HD)
    prefix_score = (
        jnp.einsum(
            "rikgd,rjkd->rkgij",
            query_block,
            cache_block[:, :, 0],
            preferred_element_type=jnp.float32,
        )
        * score_scale
    )
    suffix_score = (
        jnp.einsum(
            "rikgd,rjkd->rkgij",
            query_block,
            suffix_block[:, :, 0],
            preferred_element_type=jnp.float32,
        )
        * score_scale
    )
    positions = jnp.arange(slot_len, dtype=jnp.int32)
    allowed = (positions[None, None, :] <= positions[None, :, None]) & (
        positions[None, None, :] < suffix_len[:, None, None]
    )
    suffix_score = jnp.where(allowed[:, None, None], suffix_score, -1e30)
    score_peak = jnp.maximum(prefix_score.max(-1), suffix_score.max(-1))[..., None]
    prefix_exp = jnp.exp(prefix_score - score_peak)
    suffix_exp = jnp.exp(suffix_score - score_peak)
    normaliser = prefix_exp.sum(-1, keepdims=True) + suffix_exp.sum(-1, keepdims=True)
    prefix_prob = (prefix_exp / normaliser).astype(jnp.bfloat16)
    suffix_prob = (suffix_exp / normaliser).astype(jnp.bfloat16)
    mixed_values = jnp.einsum(
        "rkgij,rjkd->rikgd", prefix_prob, cache_block[:, :, 1], preferred_element_type=jnp.float32
    )
    mixed_values = mixed_values + jnp.einsum(
        "rkgij,rjkd->rikgd", suffix_prob, suffix_block[:, :, 1], preferred_element_type=jnp.float32
    )
    return mixed_values.reshape(requests * slot_len, kv_local * group_size * HD).astype(
        jnp.bfloat16
    )


def routing_tables(routes, live_rows, route_weight):
    expert_ids = jnp.arange(EXPERTS, dtype=jnp.int32)
    member = (routes[:, :, None] == expert_ids) & live_rows[:, None, None]
    member_int = member.astype(jnp.int32)
    flat_member = member_int.reshape(-1, EXPERTS)
    earlier = jnp.cumsum(flat_member, axis=0) - flat_member
    slot_index = jnp.sum(earlier * flat_member, axis=1).reshape(routes.shape)
    slot_hit = (slot_index[:, :, None] == jnp.arange(CAP, dtype=jnp.int32)).astype(jnp.float32)
    member_float = member.astype(jnp.float32)
    placing = (
        jnp.einsum("tke,tkc->ect", member_float, slot_hit)
        .reshape(EXPERTS * CAP, routes.shape[0])
        .astype(jnp.bfloat16)
    )
    combining = jnp.einsum(
        "tke,tkc,tk->tec", member_float, slot_hit, route_weight, precision=lax.Precision.HIGHEST
    )
    return (placing, combining.reshape(routes.shape[0], EXPERTS * CAP))


def expert_apply(arrived, w_gate, w_up, w_down):
    model_width = w_gate.shape[1]
    blocks = model_width // LANES
    packed = arrived.reshape(-1, blocks, LANES)
    gate_value = jnp.einsum(
        "rkl,klh->rh", packed, w_gate[0].reshape(blocks, LANES, -1),
        preferred_element_type=jnp.float32,
    )
    up_value = jnp.einsum(
        "rkl,klh->rh", packed, w_up[0].reshape(blocks, LANES, -1),
        preferred_element_type=jnp.float32,
    )
    hidden_units = (jax.nn.silu(gate_value) * up_value).astype(jnp.bfloat16)
    piece_out = jnp.dot(hidden_units, w_down[0], preferred_element_type=jnp.float32).astype(
        jnp.bfloat16
    )
    return piece_out.reshape(arrived.shape)


def send_back(parts):
    return lax.all_to_all(parts, "req", split_axis=0, concat_axis=0, tiled=True)


def per_device(
    queries,
    suffix_kv,
    prefix_cache,
    prefix_owner,
    request_prefix,
    suffix_len,
    residual,
    norm_gain,
    router,
    routes,
    w_gate,
    w_up,
    w_down,
    w_out,
):
    tp_count = lax.axis_size("tp")
    tp_index = lax.axis_index("tp")
    req_count = lax.axis_size("req")
    model_width = residual.shape[1]
    share_width = model_width // tp_count
    share_start = tp_index * share_width
    requests = request_prefix.shape[0]
    slot_len = queries.shape[0] // requests
    chosen = fetch_prefixes(prefix_cache, prefix_owner, request_prefix, req_count)
    attended = attend_local(queries, suffix_kv, chosen, suffix_len, requests, slot_len)
    partial_value = jnp.dot(attended, w_out, preferred_element_type=jnp.float32)
    attn_share = tp_reduce_scatter(partial_value, tp_count)
    attn_full = tp_all_gather(attn_share.astype(jnp.bfloat16), tp_count)
    hidden_state = residual.astype(jnp.float32) + attn_full.astype(jnp.float32)
    residual_share = lax.dynamic_slice_in_dim(residual, share_start, share_width, 1)
    hidden_share = residual_share.astype(jnp.float32) + attn_share
    inverse = lax.rsqrt(jnp.mean(hidden_state * hidden_state, axis=1, keepdims=True) + 1e-05)
    scaled = hidden_state * norm_gain * inverse
    logits = jnp.dot(scaled, router, precision=lax.Precision.HIGHEST)
    normed_full = scaled.astype(jnp.bfloat16)
    route_hit = (routes[:, :, None] == jnp.arange(EXPERTS, dtype=jnp.int32)).astype(jnp.float32)
    picked_logit = jnp.sum(route_hit * logits[:, None, :], axis=2)
    first_weight = jax.nn.sigmoid(picked_logit[:, 0] - picked_logit[:, 1])
    route_weight = jnp.stack([first_weight, 1.0 - first_weight], axis=1)
    live_rows = jnp.arange(routes.shape[0], dtype=jnp.int32) % slot_len < jnp.repeat(
        suffix_len, slot_len
    )
    placing, combining = routing_tables(routes, live_rows, route_weight)
    repeats = req_count // EXPERTS
    tokens = routes.shape[0]
    placing_blocks = placing.reshape(EXPERTS, CAP, tokens)
    normed_packed = normed_full.reshape(tokens, model_width // LANES, LANES)
    combining_blocks = combining.reshape(tokens, EXPERTS, CAP)
    mixture_share = jnp.zeros((tokens, share_width), jnp.float32)
    first_slot = 0
    for chunk_slots in CHUNK_SLOTS:
        packed_rows = chunk_slots * model_width // LANES
        share_rows = chunk_slots * share_width // LANES
        slots = slice(first_slot, first_slot + chunk_slots)
        first_slot += chunk_slots
        chunk_placing = jnp.tile(
            placing_blocks[:, slots].reshape(EXPERTS * chunk_slots, tokens), (repeats, 1)
        )
        send_rows = jnp.einsum(
            "ct,tkl->ckl", chunk_placing, normed_packed, preferred_element_type=jnp.float32
        ).astype(jnp.bfloat16)
        outgoing = send_rows.reshape(req_count, packed_rows, LANES)
        arrived = lax.all_to_all(outgoing, "req", split_axis=0, concat_axis=0, tiled=True)
        piece_out = expert_apply(arrived, w_gate, w_up, w_down).reshape(-1, model_width)
        reduced = lax.psum_scatter(piece_out, "tp", scatter_dimension=1, tiled=True)
        returned = send_back(reduced.reshape(req_count, share_rows, LANES))
        summed = returned.astype(jnp.float32).reshape(repeats, EXPERTS, share_rows, LANES).sum(
            axis=0
        )
        mixture_share = mixture_share + jnp.dot(
            combining_blocks[:, :, slots].reshape(tokens, EXPERTS * chunk_slots),
            summed.reshape(EXPERTS * chunk_slots, share_width),
            precision=lax.Precision.HIGHEST,
        )
    layer_out = jnp.where(live_rows[:, None], hidden_share + mixture_share, 0.0)
    return layer_out.astype(jnp.bfloat16)


def solution(mesh):
    return jax.shard_map(
        per_device,
        mesh=mesh,
        in_specs=(
            P("req", "tp"),
            P("req", None, "tp"),
            P("req", None, None, "tp"),
            P(),
            P("req"),
            P("req"),
            P("req", None),
            P(),
            P(),
            P("req", None),
            P("req", None, "tp"),
            P("req", None, "tp"),
            P("req", "tp", None),
            P("tp", None),
        ),
        out_specs=P("req", "tp"),
        check_vma=False,
    )
```
